256 devices in a mesh: gx: 16 (over y, x_hi, core), gy: 16 (over z, x_lo).
Axes of the slice: x: 4 (x_hi: 2, x_lo: 2; x = x_hi * 2 + x_lo), y: 4, z: 8, core: 2. Of those that a mesh axis runs over, the one named last changes fastest.
Arguments:
- state_field: bfloat16 [192, 256, 2048], P(None, 'gy', 'gx'), may hold values from -6 to 6
- cotangent: bfloat16 [192, 256, 2048], P(None, 'gy', 'gx'), may hold values from -6 to 6
- ocean_mask: int32 [256, 2048], P('gy', 'gx'), may hold values from 0 to 1, as said below
- kernel: float32 [192, 7, 7], replicated, may hold values from -0.875 to 0.875
- inward_weight: bfloat16 [192, 768], replicated, may hold values from -0.4375 to 0.4375
- inward_bias: float32 [768], replicated, may hold values from -3 to 3
- outward_weight: bfloat16 [768, 192], replicated, may hold values from -0.21875 to 0.21875
- layer_scale: float32 [192], replicated, may hold values from 0.1 to 1.9
Outputs:
- output_field: bfloat16 [192, 256, 2048], P(None, 'gy', 'gx')
- field_grad: bfloat16 [192, 256, 2048], P(None, 'gy', 'gx')
- kernel_grad: float32 [192, 7, 7], replicated
- inward_grad: float32 [192, 768], replicated
- outward_grad: float32 [768, 192], replicated
The draws below stay inside these ranges and needn't reach their ends.
Inputs may be any that keep to these rules, and one draw needn't show every extreme that they name: `ocean_mask`: land comes as whole blocks of 4 latitude rows by the 128 columns of one device, and as single cells.
All inputs are finite; a program needn't handle non-finite values.
Results may differ from the reference program's by a relative error of at most 0.0064.
Values may be sent and summed in bfloat16 or wider, within the bound.
No kernel may reach another device: no remote copies, remote signals or barrier semaphores. Data moves between devices by JAX's collectives and lax.ppermute only.
A program may use at most 64 MiB of HBM per device.

```python
import math
import jax
import jax.numpy as jnp
from jax import lax

C = 192
FF = 768
HT = 16
WT = 128
NLAT = 256
NLON = 2048


def draw_ocean_mask(key, part):
    block_rows = NLAT // 4
    block_cols = NLON // WT
    coarse_key = jax.random.fold_in(key, 11)
    speck_key = jax.random.fold_in(key, 12)
    coarse = jax.random.randint(coarse_key, (block_rows, block_cols), 0, 16)
    column = jnp.arange(block_cols, dtype=jnp.int32)
    limits = 2 + column % 8
    land_block = coarse < limits[None, :]
    block_full = jnp.repeat(jnp.repeat(land_block, 4, axis=0), WT, axis=1)
    speck = jax.random.randint(speck_key, (NLAT, NLON), 0, 6) == 0
    return jnp.where(block_full | speck, 0, 1).astype(jnp.int32)


def shard_levels(own_key, dims, cuts, smallest, high):
    def one(dim, shards_of):
        heights = jax.random.uniform(jax.random.fold_in(jax.random.fold_in(own_key, 6), dim), (shards_of,), jnp.float32, smallest / len(cuts), high / len(cuts))
        return jnp.repeat(jnp.exp(heights), dims[dim] // shards_of).reshape((-1,) + (1,) * (len(dims) - dim - 1))

    level = one(*cuts[0])
    for cut in cuts[1:]:
        level = level * one(*cut)
    return level


def centred(rng, extent, spread, bound, shards=(), kind=jnp.bfloat16):
    entries = spread * jax.random.normal(rng, extent, jnp.float32)
    if shards:
        entries = entries * shard_levels(rng, extent, shards, -0.22, 0.18)
    return jnp.clip(entries, -bound, bound).astype(kind)


def setup_inputs(seed: int = 0) -> dict:
    keys = jax.random.split(jax.random.key(seed), 9)
    return {
        "state_field": centred(keys[0], (C, NLAT, NLON), 1.0, 6.0, ((1, 16), (2, 16))),
        "cotangent": centred(keys[1], (C, NLAT, NLON), 1.0, 6.0, ((1, 16), (2, 16))),
        "ocean_mask": draw_ocean_mask(jax.random.fold_in(keys[8], 71), 0),
        "kernel": centred(keys[3], (C, 7, 7), 49 ** -0.5, 0.875, (), jnp.float32),
        "inward_weight": centred(keys[4], (C, FF), C ** -0.5, 0.4375),
        "inward_bias": centred(keys[5], (FF,), 0.5, 3.0, (), jnp.float32),
        "outward_weight": centred(keys[6], (FF, C), FF ** -0.5, 0.21875),
        "layer_scale": jnp.clip(1.0 + 0.18 * jax.random.normal(keys[7], (C,), jnp.float32), 0.1, 1.9),
    }


def gelu_value(values):
    return 0.5 * values * (1.0 + jax.scipy.special.erf(values / math.sqrt(2.0)))

def gelu_slope(values):
    return 0.5 * (1.0 + jax.scipy.special.erf(values / math.sqrt(2.0))) + values * jnp.exp(-0.5 * values * values) / math.sqrt(2.0 * math.pi)

def extend(source):
    wrapped = jnp.concatenate([source[:, :, -3:], source, source[:, :, :3]], axis=2)
    southern = jnp.zeros((source.shape[0], 3, wrapped.shape[2]), source.dtype)
    northern = jnp.flip(wrapped[:, -3:, :], (1, 2))
    return jnp.concatenate([southern, wrapped, northern], axis=1)

def group_conv(padded, kernel, flipped):
    lat_cells = padded.shape[1] - 6
    lon_cells = padded.shape[2] - 6
    summed = jnp.zeros((padded.shape[0], lat_cells, lon_cells), jnp.float32)
    for row_tap in range(7):
        for col_tap in range(7):
            if flipped:
                weights = kernel[:, 6 - row_tap, 6 - col_tap]
            else:
                weights = kernel[:, row_tap, col_tap]
            window = padded[:, row_tap:row_tap + lat_cells, col_tap:col_tap + lon_cells].astype(jnp.float32)
            summed = summed + weights[:, None, None] * window
    return summed

def grouped_conv(padded, kernel, flipped):
    groups = C // 16
    pad_groups = padded.reshape((groups, 16) + padded.shape[1:])
    ker_groups = kernel.reshape(groups, 16, 7, 7)
    results = lax.map(lambda operands: group_conv(operands[0], operands[1], flipped), (pad_groups, ker_groups))
    return results.reshape((C,) + results.shape[2:])

def group_kernel(grad_half, padded):
    lat_cells = grad_half.shape[1]
    lon_cells = grad_half.shape[2]
    grad_float = grad_half.astype(jnp.float32)
    row_sums = []
    for row_tap in range(7):
        column_sums = []
        for col_tap in range(7):
            window = padded[:, row_tap:row_tap + lat_cells, col_tap:col_tap + lon_cells].astype(jnp.float32)
            column_sums.append(lax.optimization_barrier(jnp.sum(grad_float * window, axis=(1, 2))))
        row_sums.append(jnp.stack(column_sums, axis=1))
    return jnp.stack(row_sums, axis=1)

def mlp_block(conv_out, field_blk, cot_blk, mask_blk, inward_weight, inward_bias, outward_weight, layer_scale):
    average = lax.optimization_barrier(jnp.mean(conv_out, axis=0, keepdims=True))
    centered = conv_out - average
    variance = lax.optimization_barrier(jnp.mean(centered * centered, axis=0, keepdims=True))
    inverse = lax.rsqrt(variance + 1e-06)
    normed = centered * inverse
    normed_half = normed.astype(jnp.bfloat16)
    contract = (((0,), (0,)), ((), ()))
    pre_act = lax.dot_general(inward_weight, normed_half, contract, preferred_element_type=jnp.float32) + inward_bias[:, None]
    hidden = gelu_value(pre_act).astype(jnp.bfloat16)
    branch = lax.dot_general(outward_weight, hidden, contract, preferred_element_type=jnp.float32)
    output_blk = (mask_blk * (field_blk.astype(jnp.float32) + layer_scale[:, None] * branch)).astype(jnp.bfloat16)
    masked_grad = mask_blk * cot_blk.astype(jnp.float32)
    branch_grad = (layer_scale[:, None] * masked_grad).astype(jnp.bfloat16)
    rows_contract = (((1,), (1,)), ((), ()))
    outward_part = lax.dot_general(hidden, branch_grad, rows_contract, preferred_element_type=jnp.float32)
    hidden_grad = jnp.dot(outward_weight, branch_grad, preferred_element_type=jnp.float32)
    pre_grad = (hidden_grad * gelu_slope(pre_act)).astype(jnp.bfloat16)
    inward_part = lax.dot_general(normed_half, pre_grad, rows_contract, preferred_element_type=jnp.float32)
    normed_grad = jnp.dot(inward_weight, pre_grad, preferred_element_type=jnp.float32)
    mean_grad = lax.optimization_barrier(jnp.mean(normed_grad, axis=0, keepdims=True))
    mean_prod = lax.optimization_barrier(jnp.mean(normed_grad * normed, axis=0, keepdims=True))
    conv_grad = (inverse * (normed_grad - mean_grad - normed * mean_prod)).astype(jnp.bfloat16)
    return (output_blk, conv_grad, inward_part, outward_part)

def reference(state_field, cotangent, ocean_mask, kernel, inward_weight, inward_bias, outward_weight, layer_scale):
    padded = extend(state_field)
    conv_out = grouped_conv(padded, kernel, False)
    mask_float = ocean_mask.astype(jnp.float32)
    block_count = NLAT // 4
    block_cells = 4 * NLON

    def scan_step(state_tuple, block_index):
        acc_in, acc_out = state_tuple
        offset = (block_index * 4).astype(jnp.int32)
        conv_blk = lax.dynamic_slice_in_dim(conv_out, offset, 4, 1).reshape(C, block_cells)
        field_blk = lax.dynamic_slice_in_dim(state_field, offset, 4, 1).reshape(C, block_cells)
        cot_blk = lax.dynamic_slice_in_dim(cotangent, offset, 4, 1).reshape(C, block_cells)
        mask_blk = lax.dynamic_slice_in_dim(mask_float, offset, 4, 0).reshape(1, block_cells)
        output_blk, conv_grad, inward_part, outward_part = mlp_block(conv_blk, field_blk, cot_blk, mask_blk, inward_weight, inward_bias, outward_weight, layer_scale)
        return ((acc_in + inward_part, acc_out + outward_part), (output_blk.reshape(C, 4, NLON), conv_grad.reshape(C, 4, NLON)))
    start_state = (jnp.zeros((C, FF), jnp.float32), jnp.zeros((FF, C), jnp.float32))
    (acc_in, acc_out), (out_blocks, grad_blocks) = lax.scan(scan_step, start_state, jnp.arange(block_count, dtype=jnp.int32))
    output_field = jnp.moveaxis(out_blocks, 0, 1).reshape(C, NLAT, NLON)
    conv_grad = jnp.moveaxis(grad_blocks, 0, 1).reshape(C, NLAT, NLON)
    factor = 1.0 / math.sqrt(HT * WT)
    grad_padded = extend(conv_grad)
    masked_grad = mask_float[None, :, :] * cotangent.astype(jnp.float32)
    field_grad = (masked_grad + grouped_conv(grad_padded, kernel, True)).astype(jnp.bfloat16)
    groups = C // 16
    grad_groups = conv_grad.reshape((groups, 16) + conv_grad.shape[1:])
    pad_groups = padded.reshape((groups, 16) + padded.shape[1:])
    kernel_parts = lax.map(lambda operands: group_kernel(operands[0], operands[1]), (grad_groups, pad_groups))
    kernel_grad = kernel_parts.reshape(C, 7, 7) * factor
    return (output_field, field_grad, kernel_grad, acc_in * factor, acc_out * factor)
```

```python
import math

import jax
import jax.numpy as jnp
from jax import lax
from jax.sharding import PartitionSpec as P


def padded_2(block, sides, width, periodic):
    for axis, dim in sides:
        count = lax.axis_size(axis)
        forward = [(i, i + 1) for i in range(count - 1)]
        if periodic:
            forward.append((count - 1, 0))
        backward = [(target, source) for source, target in forward]
        low = lax.ppermute(
            lax.slice_in_dim(block, block.shape[dim] - width, None, axis=dim), axis, forward
        )
        high = lax.ppermute(lax.slice_in_dim(block, 0, width, axis=dim), axis, backward)
        block = jnp.concatenate([low, block, high], axis=dim)
    return block


def from_partner(block, axis, distance):
    count = lax.axis_size(axis)
    route = []
    for low in range(count):
        high = low | 1 << distance
        if high != low and high < count:
            route += [(low, high), (high, low)]
    return lax.ppermute(block, axis, route)


BUTTERFLY_STEPS = (
    ("gx", 0), ("gy", 0), ("gx", 1), ("gx", 2), ("gy", 1), ("gx", 3), ("gy", 2), ("gy", 3)
)


def butterfly_sum(flat, steps):
    trail = []
    for axis, bit in steps:
        if 1 << bit >= lax.axis_size(axis):
            continue
        count = lax.axis_size(axis)
        mine = (lax.axis_index(axis) >> bit) & 1
        pairs = [(i, i ^ (1 << bit)) for i in range(count)]
        half = flat.shape[0] // 2
        low, high = flat[:half], flat[half:]
        sent = jnp.where(mine == 0, high, low)
        kept = jnp.where(mine == 0, low, high)
        flat = kept + lax.ppermute(sent, axis, pairs)
        trail.append((axis, mine, pairs))
    for axis, mine, pairs in reversed(trail):
        other = lax.ppermute(flat, axis, pairs)
        flat = jnp.where(
            mine == 0, jnp.concatenate([flat, other]), jnp.concatenate([other, flat])
        )
    return flat


def gelu_value(values):
    return 0.5 * values * (1.0 + jax.scipy.special.erf(values / math.sqrt(2.0)))


def gelu_slope(values):
    return 0.5 * (1.0 + jax.scipy.special.erf(values / math.sqrt(2.0))) + values * jnp.exp(
        -0.5 * values * values
    ) / math.sqrt(2.0 * math.pi)


def extend(source):
    lat_cells = source.shape[1]
    wrapped = padded_2(source, (("gx", 2),), 3, True)
    extended = padded_2(wrapped, (("gy", 1),), 3, False)
    top_strip = wrapped[:, lat_cells - 3 :, :]
    bit_total = lax.axis_size("gx").bit_length() - 1
    facing = top_strip
    for bit_number in range(bit_total):
        facing = from_partner(facing, "gx", bit_number)
    folded = jnp.flip(facing, (1, 2))
    at_top = lax.axis_index("gy") == lax.axis_size("gy") - 1
    upper_rows = jnp.where(at_top, folded, extended[:, lat_cells + 3 :, :])
    return jnp.concatenate([extended[:, : lat_cells + 3, :], upper_rows], axis=1)


def depthwise(padded, kernel, flipped):
    lat_cells = padded.shape[1] - 6
    lon_cells = padded.shape[2] - 6
    summed = jnp.zeros((padded.shape[0], lat_cells, lon_cells), jnp.float32)
    for row_tap in range(7):
        for col_tap in range(7):
            if flipped:
                weights = kernel[:, 6 - row_tap, 6 - col_tap]
            else:
                weights = kernel[:, row_tap, col_tap]
            window = padded[:, row_tap : row_tap + lat_cells, col_tap : col_tap + lon_cells].astype(
                jnp.float32
            )
            summed = summed + weights[:, None, None] * window
    return summed


def kernel_terms(grad_half, padded):
    lat_cells = grad_half.shape[1]
    lon_cells = grad_half.shape[2]
    grad_float = grad_half.astype(jnp.float32)
    row_sums = []
    for row_tap in range(7):
        column_sums = []
        for col_tap in range(7):
            window = padded[:, row_tap : row_tap + lat_cells, col_tap : col_tap + lon_cells].astype(
                jnp.float32
            )
            column_sums.append(jnp.sum(grad_float * window, axis=(1, 2)))
        row_sums.append(jnp.stack(column_sums, axis=1))
    return jnp.stack(row_sums, axis=1)


def mlp_block(
    conv_out, field_blk, cot_blk, mask_blk, inward_weight, inward_bias, outward_weight, layer_scale
):
    average = jnp.mean(conv_out, axis=0, keepdims=True)
    centered = conv_out - average
    variance = jnp.mean(centered * centered, axis=0, keepdims=True)
    inverse = lax.rsqrt(variance + 1e-06)
    normed = centered * inverse
    normed_half = normed.astype(jnp.bfloat16)
    contract = (((0,), (0,)), ((), ()))
    pre_act = (
        lax.dot_general(inward_weight, normed_half, contract, preferred_element_type=jnp.float32)
        + inward_bias[:, None]
    )
    hidden = gelu_value(pre_act).astype(jnp.bfloat16)
    branch = lax.dot_general(outward_weight, hidden, contract, preferred_element_type=jnp.float32)
    output_blk = (
        mask_blk * (field_blk.astype(jnp.float32) + layer_scale[:, None] * branch)
    ).astype(jnp.bfloat16)
    masked_grad = mask_blk * cot_blk.astype(jnp.float32)
    branch_grad = (layer_scale[:, None] * masked_grad).astype(jnp.bfloat16)
    rows_contract = (((1,), (1,)), ((), ()))
    outward_part = lax.dot_general(
        hidden, branch_grad, rows_contract, preferred_element_type=jnp.float32
    )
    hidden_grad = jnp.dot(outward_weight, branch_grad, preferred_element_type=jnp.float32)
    pre_grad = (hidden_grad * gelu_slope(pre_act)).astype(jnp.bfloat16)
    inward_part = lax.dot_general(
        normed_half, pre_grad, rows_contract, preferred_element_type=jnp.float32
    )
    normed_grad = jnp.dot(inward_weight, pre_grad, preferred_element_type=jnp.float32)
    mean_grad = jnp.mean(normed_grad, axis=0, keepdims=True)
    mean_prod = jnp.mean(normed_grad * normed, axis=0, keepdims=True)
    conv_grad = (inverse * (normed_grad - mean_grad - normed * mean_prod)).astype(jnp.bfloat16)
    return (output_blk, conv_grad, inward_part, outward_part)


def per_device(
    state_field,
    cotangent,
    ocean_mask,
    kernel,
    inward_weight,
    inward_bias,
    outward_weight,
    layer_scale,
):
    channels, lat_cells, lon_cells = state_field.shape
    hidden_units = inward_weight.shape[1]
    factor = 1.0 / math.sqrt(lat_cells * lon_cells)
    padded = extend(state_field)
    conv_out = depthwise(padded, kernel, False)
    block_cells = 4 * lon_cells
    block_count = lat_cells // 4
    flat_conv = conv_out.reshape(channels, lat_cells * lon_cells)
    flat_field = state_field.reshape(channels, lat_cells * lon_cells)
    flat_cot = cotangent.reshape(channels, lat_cells * lon_cells)
    mask_float = ocean_mask.astype(jnp.float32)
    flat_mask = mask_float.reshape(1, lat_cells * lon_cells)

    def block_step(block_index, state_tuple):
        out_flat, grad_flat, acc_in, acc_out = state_tuple
        offset = block_index * block_cells
        conv_blk = lax.dynamic_slice_in_dim(flat_conv, offset, block_cells, 1)
        field_blk = lax.dynamic_slice_in_dim(flat_field, offset, block_cells, 1)
        cot_blk = lax.dynamic_slice_in_dim(flat_cot, offset, block_cells, 1)
        mask_blk = lax.dynamic_slice_in_dim(flat_mask, offset, block_cells, 1)

        def compute_block(unused):
            return mlp_block(
                conv_blk,
                field_blk,
                cot_blk,
                mask_blk,
                inward_weight,
                inward_bias,
                outward_weight,
                layer_scale,
            )

        def skip_block(unused):
            zero_half = jnp.zeros((channels, block_cells), jnp.bfloat16)
            return (
                zero_half,
                zero_half,
                jnp.zeros((channels, hidden_units), jnp.float32),
                jnp.zeros((hidden_units, channels), jnp.float32),
            )

        output_blk, conv_grad, inward_part, outward_part = lax.cond(
            jnp.max(mask_blk) > 0.0, compute_block, skip_block, None
        )
        out_flat = lax.dynamic_update_slice_in_dim(out_flat, output_blk, offset, 1)
        grad_flat = lax.dynamic_update_slice_in_dim(grad_flat, conv_grad, offset, 1)
        return (out_flat, grad_flat, acc_in + inward_part, acc_out + outward_part)

    start_state = (
        jnp.zeros((channels, lat_cells * lon_cells), jnp.bfloat16),
        jnp.zeros((channels, lat_cells * lon_cells), jnp.bfloat16),
        jnp.zeros((channels, hidden_units), jnp.float32),
        jnp.zeros((hidden_units, channels), jnp.float32),
    )
    out_flat, grad_flat, acc_in, acc_out = lax.fori_loop(0, block_count, block_step, start_state)
    output_field = out_flat.reshape(channels, lat_cells, lon_cells)
    conv_grad = grad_flat.reshape(channels, lat_cells, lon_cells)
    kernel_local = kernel_terms(conv_grad, padded) * factor
    parts = (acc_in * factor, acc_out * factor, kernel_local)
    flat = jnp.concatenate([part.reshape(-1) for part in parts])
    total = flat.shape[0]
    padded_total = -(-total // 2048) * 2048
    flat = jnp.pad(flat, (0, padded_total - total))
    flat = butterfly_sum(flat, BUTTERFLY_STEPS)
    sums = []
    start = 0
    for part in parts:
        sums.append(flat[start : start + part.size].reshape(part.shape))
        start += part.size
    inward_grad, outward_grad, kernel_grad = sums
    grad_padded = extend(conv_grad)
    masked_grad = mask_float[None, :, :] * cotangent.astype(jnp.float32)
    field_grad = (masked_grad + depthwise(grad_padded, kernel, True)).astype(jnp.bfloat16)
    return (output_field, field_grad, kernel_grad, inward_grad, outward_grad)


def solution(mesh):
    in_specs = (P(None, "gy", "gx"), P(None, "gy", "gx"), P("gy", "gx"), P(), P(), P(), P(), P())
    out_specs = (P(None, "gy", "gx"), P(None, "gy", "gx"), P(), P(), P())
    return jax.shard_map(
        per_device, mesh=mesh, in_specs=in_specs, out_specs=out_specs, check_vma=False
    )
```

```python
import math

import jax
import jax.numpy as jnp
from jax import lax
from jax.sharding import PartitionSpec as P
from jax.experimental import pallas as pl
from jax.experimental.pallas import tpu as pltpu


def padded_2(block, sides, width, periodic):
    for axis, dim in sides:
        count = lax.axis_size(axis)
        forward = [(i, i + 1) for i in range(count - 1)]
        if periodic:
            forward.append((count - 1, 0))
        backward = [(target, source) for source, target in forward]
        low = lax.ppermute(
            lax.slice_in_dim(block, block.shape[dim] - width, None, axis=dim), axis, forward
        )
        high = lax.ppermute(lax.slice_in_dim(block, 0, width, axis=dim), axis, backward)
        block = jnp.concatenate([low, block, high], axis=dim)
    return block


def from_partner(block, axis, distance):
    count = lax.axis_size(axis)
    route = []
    for low in range(count):
        high = low | 1 << distance
        if high != low and high < count:
            route += [(low, high), (high, low)]
    return lax.ppermute(block, axis, route)


BUTTERFLY_STEPS = (
    ("gx", 0), ("gy", 0), ("gx", 1), ("gx", 2), ("gy", 1), ("gx", 3), ("gy", 2), ("gy", 3)
)


def butterfly_sum(flat, steps):
    trail = []
    for axis, bit in steps:
        if 1 << bit >= lax.axis_size(axis):
            continue
        count = lax.axis_size(axis)
        mine = (lax.axis_index(axis) >> bit) & 1
        pairs = [(i, i ^ (1 << bit)) for i in range(count)]
        half = flat.shape[0] // 2
        low, high = flat[:half], flat[half:]
        sent = jnp.where(mine == 0, high, low)
        kept = jnp.where(mine == 0, low, high)
        flat = kept + lax.ppermute(sent, axis, pairs)
        trail.append((axis, mine, pairs))
    for axis, mine, pairs in reversed(trail):
        other = lax.ppermute(flat, axis, pairs)
        flat = jnp.where(
            mine == 0, jnp.concatenate([flat, other]), jnp.concatenate([other, flat])
        )
    return flat


def gelu_value(values):
    return 0.5 * values * (1.0 + jax.scipy.special.erf(values / math.sqrt(2.0)))


def gelu_slope(values):
    return 0.5 * (1.0 + jax.scipy.special.erf(values / math.sqrt(2.0))) + values * jnp.exp(
        -0.5 * values * values
    ) / math.sqrt(2.0 * math.pi)


def extend(source):
    lat_cells = source.shape[1]
    wrapped = padded_2(source, (("gx", 2),), 3, True)
    extended = padded_2(wrapped, (("gy", 1),), 3, False)
    top_strip = wrapped[:, lat_cells - 3 :, :]
    count = lax.axis_size("gx")
    facing = lax.ppermute(top_strip, "gx", [(i, count - 1 - i) for i in range(count)])
    folded = jnp.flip(facing, (1, 2))
    at_top = lax.axis_index("gy") == lax.axis_size("gy") - 1
    upper_rows = jnp.where(at_top, folded, extended[:, lat_cells + 3 :, :])
    return jnp.concatenate([extended[:, : lat_cells + 3, :], upper_rows], axis=1)


def depthwise(padded, kernel, flipped):
    lat_cells = padded.shape[1] - 6
    lon_cells = padded.shape[2] - 6
    summed = jnp.zeros((padded.shape[0], lat_cells, lon_cells), jnp.float32)
    for row_tap in range(7):
        for col_tap in range(7):
            if flipped:
                weights = kernel[:, 6 - row_tap, 6 - col_tap]
            else:
                weights = kernel[:, row_tap, col_tap]
            window = padded[:, row_tap : row_tap + lat_cells, col_tap : col_tap + lon_cells].astype(
                jnp.float32
            )
            summed = summed + weights[:, None, None] * window
    return summed


def kernel_terms(grad_half, padded):
    lat_cells = grad_half.shape[1]
    lon_cells = grad_half.shape[2]
    grad_float = grad_half.astype(jnp.float32)
    row_sums = []
    for row_tap in range(7):
        column_sums = []
        for col_tap in range(7):
            window = padded[:, row_tap : row_tap + lat_cells, col_tap : col_tap + lon_cells].astype(
                jnp.float32
            )
            column_sums.append(jnp.sum(grad_float * window, axis=(1, 2)))
        row_sums.append(jnp.stack(column_sums, axis=1))
    return jnp.stack(row_sums, axis=1)


def mlp_block(
    conv_out, field_blk, cot_blk, mask_blk, inward_weight, inward_bias, outward_weight, layer_scale
):
    average = jnp.mean(conv_out, axis=0, keepdims=True)
    centered = conv_out - average
    variance = jnp.mean(centered * centered, axis=0, keepdims=True)
    inverse = lax.rsqrt(variance + 1e-06)
    normed = centered * inverse
    normed_half = normed.astype(jnp.bfloat16)
    contract = (((0,), (0,)), ((), ()))
    pre_act = (
        lax.dot_general(inward_weight, normed_half, contract, preferred_element_type=jnp.float32)
        + inward_bias[:, None]
    )
    hidden = gelu_value(pre_act).astype(jnp.bfloat16)
    branch = lax.dot_general(outward_weight, hidden, contract, preferred_element_type=jnp.float32)
    output_blk = (
        mask_blk * (field_blk.astype(jnp.float32) + layer_scale[:, None] * branch)
    ).astype(jnp.bfloat16)
    masked_grad = mask_blk * cot_blk.astype(jnp.float32)
    branch_grad = (layer_scale[:, None] * masked_grad).astype(jnp.bfloat16)
    rows_contract = (((1,), (1,)), ((), ()))
    outward_part = lax.dot_general(
        hidden, branch_grad, rows_contract, preferred_element_type=jnp.float32
    )
    hidden_grad = jnp.dot(outward_weight, branch_grad, preferred_element_type=jnp.float32)
    pre_grad = (hidden_grad * gelu_slope(pre_act)).astype(jnp.bfloat16)
    inward_part = lax.dot_general(
        normed_half, pre_grad, rows_contract, preferred_element_type=jnp.float32
    )
    normed_grad = jnp.dot(inward_weight, pre_grad, preferred_element_type=jnp.float32)
    mean_grad = jnp.mean(normed_grad, axis=0, keepdims=True)
    mean_prod = jnp.mean(normed_grad * normed, axis=0, keepdims=True)
    conv_grad = (inverse * (normed_grad - mean_grad - normed * mean_prod)).astype(jnp.bfloat16)
    return (output_blk, conv_grad, inward_part, outward_part)


TILE = 512


def mlp_kernel(
    conv_ref, field_ref, cot_ref, mask_ref, win_t_ref, win_ref, wout_ref, wout_t_ref,
    bias_ref, scale_ref, out_ref, grad_ref, acc_in_ref, acc_out_ref,
):
    @pl.when(pl.program_id(0) == 0)
    def _():
        acc_in_ref[...] = jnp.zeros_like(acc_in_ref)
        acc_out_ref[...] = jnp.zeros_like(acc_out_ref)

    conv = conv_ref[...]
    channels = conv.shape[0]
    average = jnp.sum(conv, axis=0, keepdims=True) / channels
    centered = conv - average
    variance = jnp.sum(centered * centered, axis=0, keepdims=True) / channels
    inverse = lax.rsqrt(variance + 1e-06)
    normed = centered * inverse
    normed_half = normed.astype(jnp.bfloat16)
    pre_act = jnp.dot(win_t_ref[...], normed_half, preferred_element_type=jnp.float32)
    pre_act = pre_act + bias_ref[...]
    hidden = gelu_value(pre_act).astype(jnp.bfloat16)
    branch = jnp.dot(wout_t_ref[...], hidden, preferred_element_type=jnp.float32)
    mask = mask_ref[...]
    scale = scale_ref[...]
    out_ref[...] = (
        mask * (field_ref[...].astype(jnp.float32) + scale * branch)
    ).astype(out_ref.dtype)
    masked_grad = mask * cot_ref[...].astype(jnp.float32)
    branch_grad = (scale * masked_grad).astype(jnp.bfloat16)
    rows_contract = (((1,), (1,)), ((), ()))
    acc_out_ref[...] += lax.dot_general(
        hidden, branch_grad, rows_contract, preferred_element_type=jnp.float32
    )
    hidden_grad = jnp.dot(wout_ref[...], branch_grad, preferred_element_type=jnp.float32)
    pre_grad = (hidden_grad * gelu_slope(pre_act)).astype(jnp.bfloat16)
    acc_in_ref[...] += lax.dot_general(
        normed_half, pre_grad, rows_contract, preferred_element_type=jnp.float32
    )
    normed_grad = jnp.dot(win_ref[...], pre_grad, preferred_element_type=jnp.float32)
    mean_grad = jnp.sum(normed_grad, axis=0, keepdims=True) / channels
    mean_prod = jnp.sum(normed_grad * normed, axis=0, keepdims=True) / channels
    grad_ref[...] = (inverse * (normed_grad - mean_grad - normed * mean_prod)).astype(
        grad_ref.dtype
    )


def fused_mlp(conv, field, cot, mask, inward_weight, inward_bias, outward_weight, layer_scale):
    channels, cells = conv.shape
    hidden_units = inward_weight.shape[1]
    tile = TILE if cells % TILE == 0 else cells
    steps = cells // tile
    cell_block = lambda rows: pl.BlockSpec((rows, tile), lambda i: (0, i))
    whole = lambda shape: pl.BlockSpec(shape, lambda i: (0, 0))
    flops = 2 * 6 * channels * hidden_units * cells
    return pl.pallas_call(
        mlp_kernel,
        grid=(steps,),
        in_specs=[
            cell_block(channels), cell_block(channels), cell_block(channels), cell_block(1),
            whole((hidden_units, channels)), whole((channels, hidden_units)),
            whole((hidden_units, channels)), whole((channels, hidden_units)),
            whole((hidden_units, 1)), whole((channels, 1)),
        ],
        out_specs=[
            cell_block(channels), cell_block(channels),
            whole((channels, hidden_units)), whole((hidden_units, channels)),
        ],
        out_shape=[
            jax.ShapeDtypeStruct((channels, cells), jnp.bfloat16),
            jax.ShapeDtypeStruct((channels, cells), jnp.bfloat16),
            jax.ShapeDtypeStruct((channels, hidden_units), jnp.float32),
            jax.ShapeDtypeStruct((hidden_units, channels), jnp.float32),
        ],
        compiler_params=pltpu.CompilerParams(dimension_semantics=("arbitrary",)),
        cost_estimate=pl.CostEstimate(
            flops=flops, transcendentals=3 * hidden_units * cells,
            bytes_accessed=channels * cells * 12,
        ),
    )(
        conv, field, cot, mask, inward_weight.T, inward_weight, outward_weight,
        outward_weight.T, inward_bias.reshape(hidden_units, 1),
        layer_scale.reshape(channels, 1),
    )


def per_device(
    state_field,
    cotangent,
    ocean_mask,
    kernel,
    inward_weight,
    inward_bias,
    outward_weight,
    layer_scale,
):
    channels, lat_cells, lon_cells = state_field.shape
    hidden_units = inward_weight.shape[1]
    factor = 1.0 / math.sqrt(lat_cells * lon_cells)
    padded = extend(state_field)
    conv_out = depthwise(padded, kernel, False)
    cells = lat_cells * lon_cells
    flat_conv = conv_out.reshape(channels, cells)
    flat_field = state_field.reshape(channels, cells)
    flat_cot = cotangent.reshape(channels, cells)
    mask_float = ocean_mask.astype(jnp.float32)
    flat_mask = mask_float.reshape(1, cells)
    out_flat, grad_flat, acc_in, acc_out = fused_mlp(
        flat_conv, flat_field, flat_cot, flat_mask,
        inward_weight, inward_bias, outward_weight, layer_scale,
    )
    output_field = out_flat.reshape(channels, lat_cells, lon_cells)
    conv_grad = grad_flat.reshape(channels, lat_cells, lon_cells)
    kernel_local = kernel_terms(conv_grad, padded) * factor
    parts = (acc_in * factor, acc_out * factor, kernel_local)
    flat = jnp.concatenate([part.reshape(-1) for part in parts])
    total = flat.shape[0]
    padded_total = -(-total // 2048) * 2048
    flat = jnp.pad(flat, (0, padded_total - total))
    flat = butterfly_sum(flat, BUTTERFLY_STEPS)
    sums = []
    start = 0
    for part in parts:
        sums.append(flat[start : start + part.size].reshape(part.shape))
        start += part.size
    inward_grad, outward_grad, kernel_grad = sums
    grad_padded = extend(conv_grad)
    masked_grad = mask_float[None, :, :] * cotangent.astype(jnp.float32)
    field_grad = (masked_grad + depthwise(grad_padded, kernel, True)).astype(jnp.bfloat16)
    return (output_field, field_grad, kernel_grad, inward_grad, outward_grad)


def solution(mesh):
    in_specs = (P(None, "gy", "gx"), P(None, "gy", "gx"), P("gy", "gx"), P(), P(), P(), P(), P())
    out_specs = (P(None, "gy", "gx"), P(None, "gy", "gx"), P(), P(), P())
    return jax.shard_map(
        per_device, mesh=mesh, in_specs=in_specs, out_specs=out_specs, check_vma=False
    )
```

```python
import math

import jax
import jax.numpy as jnp
from jax import lax
from jax.sharding import PartitionSpec as P
from jax.experimental import pallas as pl
from jax.experimental.pallas import tpu as pltpu


def padded_2(block, sides, width, periodic):
    for axis, dim in sides:
        count = lax.axis_size(axis)
        forward = [(i, i + 1) for i in range(count - 1)]
        if periodic:
            forward.append((count - 1, 0))
        backward = [(target, source) for source, target in forward]
        low = lax.ppermute(
            lax.slice_in_dim(block, block.shape[dim] - width, None, axis=dim), axis, forward
        )
        high = lax.ppermute(lax.slice_in_dim(block, 0, width, axis=dim), axis, backward)
        block = jnp.concatenate([low, block, high], axis=dim)
    return block


BUTTERFLY_STEPS = (
    ("gx", 0), ("gy", 0), ("gx", 1), ("gx", 2), ("gy", 1), ("gx", 3), ("gy", 2), ("gy", 3)
)


def butterfly_sum(flat, steps):
    trail = []
    for axis, bit in steps:
        if 1 << bit >= lax.axis_size(axis):
            continue
        count = lax.axis_size(axis)
        mine = (lax.axis_index(axis) >> bit) & 1
        pairs = [(i, i ^ (1 << bit)) for i in range(count)]
        half = flat.shape[0] // 2
        low, high = flat[:half], flat[half:]
        sent = jnp.where(mine == 0, high, low)
        kept = jnp.where(mine == 0, low, high)
        flat = kept + lax.ppermute(sent, axis, pairs)
        trail.append((axis, mine, pairs))
    for axis, mine, pairs in reversed(trail):
        other = lax.ppermute(flat, axis, pairs)
        flat = jnp.where(
            mine == 0, jnp.concatenate([flat, other]), jnp.concatenate([other, flat])
        )
    return flat


def gelu_value(values):
    return 0.5 * values * (1.0 + jax.scipy.special.erf(values / math.sqrt(2.0)))


def gelu_slope(values):
    return 0.5 * (1.0 + jax.scipy.special.erf(values / math.sqrt(2.0))) + values * jnp.exp(
        -0.5 * values * values
    ) / math.sqrt(2.0 * math.pi)


def extend(source):
    lat_cells = source.shape[1]
    wrapped = padded_2(source, (("gx", 2),), 3, True)
    extended = padded_2(wrapped, (("gy", 1),), 3, False)
    top_strip = wrapped[:, lat_cells - 3 :, :]
    count = lax.axis_size("gx")
    facing = lax.ppermute(top_strip, "gx", [(i, count - 1 - i) for i in range(count)])
    folded = jnp.flip(facing, (1, 2))
    at_top = lax.axis_index("gy") == lax.axis_size("gy") - 1
    upper_rows = jnp.where(at_top, folded, extended[:, lat_cells + 3 :, :])
    return jnp.concatenate([extended[:, : lat_cells + 3, :], upper_rows], axis=1)


def depthwise(padded, kernel, flipped):
    lat_cells = padded.shape[1] - 6
    lon_cells = padded.shape[2] - 6
    summed = jnp.zeros((padded.shape[0], lat_cells, lon_cells), jnp.float32)
    for row_tap in range(7):
        for col_tap in range(7):
            if flipped:
                weights = kernel[:, 6 - row_tap, 6 - col_tap]
            else:
                weights = kernel[:, row_tap, col_tap]
            window = padded[:, row_tap : row_tap + lat_cells, col_tap : col_tap + lon_cells].astype(
                jnp.float32
            )
            summed = summed + weights[:, None, None] * window
    return summed


def kernel_terms(grad_half, padded):
    lat_cells = grad_half.shape[1]
    lon_cells = grad_half.shape[2]
    grad_float = grad_half.astype(jnp.float32)
    row_sums = []
    for row_tap in range(7):
        column_sums = []
        for col_tap in range(7):
            window = padded[:, row_tap : row_tap + lat_cells, col_tap : col_tap + lon_cells].astype(
                jnp.float32
            )
            column_sums.append(jnp.sum(grad_float * window, axis=(1, 2)))
        row_sums.append(jnp.stack(column_sums, axis=1))
    return jnp.stack(row_sums, axis=1)


TILE = 512


def mlp_kernel(
    conv_ref, field_ref, cot_ref, mask_ref, win_t_ref, win_ref, wout_ref, wout_t_ref,
    bias_ref, scale_ref, out_ref, grad_ref, acc_in_ref, acc_out_ref,
):
    @pl.when(pl.program_id(0) == 0)
    def _():
        acc_in_ref[...] = jnp.zeros_like(acc_in_ref)
        acc_out_ref[...] = jnp.zeros_like(acc_out_ref)

    conv = conv_ref[...]
    channels = conv.shape[0]
    average = jnp.sum(conv, axis=0, keepdims=True) / channels
    centered = conv - average
    variance = jnp.sum(centered * centered, axis=0, keepdims=True) / channels
    inverse = lax.rsqrt(variance + 1e-06)
    normed = centered * inverse
    normed_half = normed.astype(jnp.bfloat16)
    pre_act = jnp.dot(win_t_ref[...], normed_half, preferred_element_type=jnp.float32)
    pre_act = pre_act + bias_ref[...]
    hidden = gelu_value(pre_act).astype(jnp.bfloat16)
    branch = jnp.dot(wout_t_ref[...], hidden, preferred_element_type=jnp.float32)
    mask = mask_ref[...]
    scale = scale_ref[...]
    out_ref[...] = (
        mask * (field_ref[...].astype(jnp.float32) + scale * branch)
    ).astype(out_ref.dtype)
    masked_grad = mask * cot_ref[...].astype(jnp.float32)
    branch_grad = (scale * masked_grad).astype(jnp.bfloat16)
    rows_contract = (((1,), (1,)), ((), ()))
    acc_out_ref[...] += lax.dot_general(
        hidden, branch_grad, rows_contract, preferred_element_type=jnp.float32
    )
    hidden_grad = jnp.dot(wout_ref[...], branch_grad, preferred_element_type=jnp.float32)
    pre_grad = (hidden_grad * gelu_slope(pre_act)).astype(jnp.bfloat16)
    acc_in_ref[...] += lax.dot_general(
        normed_half, pre_grad, rows_contract, preferred_element_type=jnp.float32
    )
    normed_grad = jnp.dot(win_ref[...], pre_grad, preferred_element_type=jnp.float32)
    mean_grad = jnp.sum(normed_grad, axis=0, keepdims=True) / channels
    mean_prod = jnp.sum(normed_grad * normed, axis=0, keepdims=True) / channels
    grad_ref[...] = (inverse * (normed_grad - mean_grad - normed * mean_prod)).astype(
        grad_ref.dtype
    )


def fused_mlp(conv, field, cot, mask, inward_weight, inward_bias, outward_weight, layer_scale):
    channels, cells = conv.shape
    hidden_units = inward_weight.shape[1]
    tile = TILE if cells % TILE == 0 else cells
    steps = cells // tile
    cell_block = lambda rows: pl.BlockSpec((rows, tile), lambda i: (0, i))
    whole = lambda shape: pl.BlockSpec(shape, lambda i: (0, 0))
    flops = 2 * 6 * channels * hidden_units * cells
    return pl.pallas_call(
        mlp_kernel,
        grid=(steps,),
        in_specs=[
            cell_block(channels), cell_block(channels), cell_block(channels), cell_block(1),
            whole((hidden_units, channels)), whole((channels, hidden_units)),
            whole((hidden_units, channels)), whole((channels, hidden_units)),
            whole((hidden_units, 1)), whole((channels, 1)),
        ],
        out_specs=[
            cell_block(channels), cell_block(channels),
            whole((channels, hidden_units)), whole((hidden_units, channels)),
        ],
        out_shape=[
            jax.ShapeDtypeStruct((channels, cells), jnp.bfloat16),
            jax.ShapeDtypeStruct((channels, cells), jnp.bfloat16),
            jax.ShapeDtypeStruct((channels, hidden_units), jnp.float32),
            jax.ShapeDtypeStruct((hidden_units, channels), jnp.float32),
        ],
        compiler_params=pltpu.CompilerParams(dimension_semantics=("arbitrary",)),
        cost_estimate=pl.CostEstimate(
            flops=flops, transcendentals=3 * hidden_units * cells,
            bytes_accessed=channels * cells * 12,
        ),
    )(
        conv, field, cot, mask, inward_weight.T, inward_weight, outward_weight,
        outward_weight.T, inward_bias.reshape(hidden_units, 1),
        layer_scale.reshape(channels, 1),
    )


def per_device(
    state_field,
    cotangent,
    ocean_mask,
    kernel,
    inward_weight,
    inward_bias,
    outward_weight,
    layer_scale,
):
    channels, lat_cells, lon_cells = state_field.shape
    factor = 1.0 / math.sqrt(lat_cells * lon_cells)
    padded = extend(state_field)
    conv_out = depthwise(padded, kernel, False)
    cells = lat_cells * lon_cells
    flat_conv = conv_out.reshape(channels, cells)
    flat_field = state_field.reshape(channels, cells)
    flat_cot = cotangent.reshape(channels, cells)
    mask_float = ocean_mask.astype(jnp.float32)
    flat_mask = mask_float.reshape(1, cells)
    out_flat, grad_flat, acc_in, acc_out = fused_mlp(
        flat_conv, flat_field, flat_cot, flat_mask,
        inward_weight, inward_bias, outward_weight, layer_scale,
    )
    output_field = out_flat.reshape(channels, lat_cells, lon_cells)
    conv_grad = grad_flat.reshape(channels, lat_cells, lon_cells)
    kernel_local = kernel_terms(conv_grad, padded) * factor
    parts = (acc_in * factor, acc_out * factor, kernel_local)
    flat = jnp.concatenate([part.reshape(-1) for part in parts])
    total = flat.shape[0]
    padded_total = -(-total // 2048) * 2048
    flat = jnp.pad(flat, (0, padded_total - total))
    flat = butterfly_sum(flat, BUTTERFLY_STEPS)
    sums = []
    start = 0
    for part in parts:
        sums.append(flat[start : start + part.size].reshape(part.shape))
        start += part.size
    inward_grad, outward_grad, kernel_grad = sums
    grad_padded = extend(conv_grad)
    masked_grad = mask_float[None, :, :] * cotangent.astype(jnp.float32)
    field_grad = (masked_grad + depthwise(grad_padded, kernel, True)).astype(jnp.bfloat16)
    return (output_field, field_grad, kernel_grad, inward_grad, outward_grad)


def solution(mesh):
    in_specs = (P(None, "gy", "gx"), P(None, "gy", "gx"), P("gy", "gx"), P(), P(), P(), P(), P())
    out_specs = (P(None, "gy", "gx"), P(None, "gy", "gx"), P(), P(), P())
    return jax.shard_map(
        per_device, mesh=mesh, in_specs=in_specs, out_specs=out_specs, check_vma=False
    )
```

```python
import math

import jax
import jax.numpy as jnp
from jax import lax
from jax.sharding import PartitionSpec as P
from jax.experimental import pallas as pl
from jax.experimental.pallas import tpu as pltpu


def padded_2(block, sides, width, periodic):
    for axis, dim in sides:
        count = lax.axis_size(axis)
        forward = [(i, i + 1) for i in range(count - 1)]
        if periodic:
            forward.append((count - 1, 0))
        backward = [(target, source) for source, target in forward]
        low = lax.ppermute(
            lax.slice_in_dim(block, block.shape[dim] - width, None, axis=dim), axis, forward
        )
        high = lax.ppermute(lax.slice_in_dim(block, 0, width, axis=dim), axis, backward)
        block = jnp.concatenate([low, block, high], axis=dim)
    return block


BUTTERFLY_BITS = (
    ("gx", 0), ("gy", 0), ("gx", 1), ("gx", 2), ("gy", 1), ("gx", 3), ("gy", 2), ("gy", 3)
)
AXES = ("gx", "gy")


def butterfly_sum(flat, bits):
    inner = lax.axis_size("gy").bit_length() - 1
    count = lax.axis_size("gx") * lax.axis_size("gy")
    linear = [bit + (inner if axis == "gx" else 0) for axis, bit in bits if 1 << bit < lax.axis_size(axis)]
    groups = [tuple(linear[i : i + 2]) for i in range(0, len(linear), 2)]
    me = lax.axis_index(AXES)
    trail = []
    for group in groups:
        ways = 1 << len(group)
        mine = sum(((me >> bit) & 1) << place for place, bit in enumerate(group))
        share = flat.shape[0] // ways
        total = lax.dynamic_slice_in_dim(flat, mine * share, share)
        for other in range(1, ways):
            mask = sum(((other >> place) & 1) << bit for place, bit in enumerate(group))
            pairs = [(i, i ^ mask) for i in range(count)]
            sent = lax.dynamic_slice_in_dim(flat, (mine ^ other) * share, share)
            total = total + lax.ppermute(sent, AXES, pairs)
        flat = total
        trail.append((group, mine))
    for group, mine in reversed(trail):
        ways = 1 << len(group)
        share = flat.shape[0]
        whole = jnp.zeros((ways * share,), flat.dtype)
        whole = lax.dynamic_update_slice_in_dim(whole, flat, mine * share, 0)
        for other in range(1, ways):
            mask = sum(((other >> place) & 1) << bit for place, bit in enumerate(group))
            pairs = [(i, i ^ mask) for i in range(count)]
            got = lax.ppermute(flat, AXES, pairs)
            whole = lax.dynamic_update_slice_in_dim(whole, got, (mine ^ other) * share, 0)
        flat = whole
    return flat


def gelu_value(values):
    return 0.5 * values * (1.0 + jax.scipy.special.erf(values / math.sqrt(2.0)))


def gelu_slope(values):
    return 0.5 * (1.0 + jax.scipy.special.erf(values / math.sqrt(2.0))) + values * jnp.exp(
        -0.5 * values * values
    ) / math.sqrt(2.0 * math.pi)


def extend(source):
    lat_cells = source.shape[1]
    wrapped = padded_2(source, (("gx", 2),), 3, True)
    extended = padded_2(wrapped, (("gy", 1),), 3, False)
    top_strip = wrapped[:, lat_cells - 3 :, :]
    count = lax.axis_size("gx")
    facing = lax.ppermute(top_strip, "gx", [(i, count - 1 - i) for i in range(count)])
    folded = jnp.flip(facing, (1, 2))
    at_top = lax.axis_index("gy") == lax.axis_size("gy") - 1
    upper_rows = jnp.where(at_top, folded, extended[:, lat_cells + 3 :, :])
    return jnp.concatenate([extended[:, : lat_cells + 3, :], upper_rows], axis=1)


def depthwise(padded, kernel, flipped):
    lat_cells = padded.shape[1] - 6
    lon_cells = padded.shape[2] - 6
    summed = jnp.zeros((padded.shape[0], lat_cells, lon_cells), jnp.float32)
    for row_tap in range(7):
        for col_tap in range(7):
            if flipped:
                weights = kernel[:, 6 - row_tap, 6 - col_tap]
            else:
                weights = kernel[:, row_tap, col_tap]
            window = padded[:, row_tap : row_tap + lat_cells, col_tap : col_tap + lon_cells].astype(
                jnp.float32
            )
            summed = summed + weights[:, None, None] * window
    return summed


def kernel_terms(grad_half, padded):
    lat_cells = grad_half.shape[1]
    lon_cells = grad_half.shape[2]
    grad_float = grad_half.astype(jnp.float32)
    row_sums = []
    for row_tap in range(7):
        column_sums = []
        for col_tap in range(7):
            window = padded[:, row_tap : row_tap + lat_cells, col_tap : col_tap + lon_cells].astype(
                jnp.float32
            )
            column_sums.append(jnp.sum(grad_float * window, axis=(1, 2)))
        row_sums.append(jnp.stack(column_sums, axis=1))
    return jnp.stack(row_sums, axis=1)


TILE = 512


def mlp_kernel(
    conv_ref, field_ref, cot_ref, mask_ref, win_t_ref, win_ref, wout_ref, wout_t_ref,
    bias_ref, scale_ref, out_ref, grad_ref, acc_in_ref, acc_out_ref,
):
    @pl.when(pl.program_id(0) == 0)
    def _():
        acc_in_ref[...] = jnp.zeros_like(acc_in_ref)
        acc_out_ref[...] = jnp.zeros_like(acc_out_ref)

    conv = conv_ref[...]
    channels = conv.shape[0]
    average = jnp.sum(conv, axis=0, keepdims=True) / channels
    centered = conv - average
    variance = jnp.sum(centered * centered, axis=0, keepdims=True) / channels
    inverse = lax.rsqrt(variance + 1e-06)
    normed = centered * inverse
    normed_half = normed.astype(jnp.bfloat16)
    pre_act = jnp.dot(win_t_ref[...], normed_half, preferred_element_type=jnp.float32)
    pre_act = pre_act + bias_ref[...]
    hidden = gelu_value(pre_act).astype(jnp.bfloat16)
    branch = jnp.dot(wout_t_ref[...], hidden, preferred_element_type=jnp.float32)
    mask = mask_ref[...]
    scale = scale_ref[...]
    out_ref[...] = (
        mask * (field_ref[...].astype(jnp.float32) + scale * branch)
    ).astype(out_ref.dtype)
    masked_grad = mask * cot_ref[...].astype(jnp.float32)
    branch_grad = (scale * masked_grad).astype(jnp.bfloat16)
    rows_contract = (((1,), (1,)), ((), ()))
    acc_out_ref[...] += lax.dot_general(
        hidden, branch_grad, rows_contract, preferred_element_type=jnp.float32
    )
    hidden_grad = jnp.dot(wout_ref[...], branch_grad, preferred_element_type=jnp.float32)
    pre_grad = (hidden_grad * gelu_slope(pre_act)).astype(jnp.bfloat16)
    acc_in_ref[...] += lax.dot_general(
        normed_half, pre_grad, rows_contract, preferred_element_type=jnp.float32
    )
    normed_grad = jnp.dot(win_ref[...], pre_grad, preferred_element_type=jnp.float32)
    mean_grad = jnp.sum(normed_grad, axis=0, keepdims=True) / channels
    mean_prod = jnp.sum(normed_grad * normed, axis=0, keepdims=True) / channels
    grad_ref[...] = (inverse * (normed_grad - mean_grad - normed * mean_prod)).astype(
        grad_ref.dtype
    )


def fused_mlp(conv, field, cot, mask, inward_weight, inward_bias, outward_weight, layer_scale):
    channels, cells = conv.shape
    hidden_units = inward_weight.shape[1]
    tile = TILE if cells % TILE == 0 else cells
    steps = cells // tile
    cell_block = lambda rows: pl.BlockSpec((rows, tile), lambda i: (0, i))
    whole = lambda shape: pl.BlockSpec(shape, lambda i: (0, 0))
    flops = 2 * 6 * channels * hidden_units * cells
    return pl.pallas_call(
        mlp_kernel,
        grid=(steps,),
        in_specs=[
            cell_block(channels), cell_block(channels), cell_block(channels), cell_block(1),
            whole((hidden_units, channels)), whole((channels, hidden_units)),
            whole((hidden_units, channels)), whole((channels, hidden_units)),
            whole((hidden_units, 1)), whole((channels, 1)),
        ],
        out_specs=[
            cell_block(channels), cell_block(channels),
            whole((channels, hidden_units)), whole((hidden_units, channels)),
        ],
        out_shape=[
            jax.ShapeDtypeStruct((channels, cells), jnp.bfloat16),
            jax.ShapeDtypeStruct((channels, cells), jnp.bfloat16),
            jax.ShapeDtypeStruct((channels, hidden_units), jnp.float32),
            jax.ShapeDtypeStruct((hidden_units, channels), jnp.float32),
        ],
        compiler_params=pltpu.CompilerParams(dimension_semantics=("arbitrary",)),
        cost_estimate=pl.CostEstimate(
            flops=flops, transcendentals=3 * hidden_units * cells,
            bytes_accessed=channels * cells * 12,
        ),
    )(
        conv, field, cot, mask, inward_weight.T, inward_weight, outward_weight,
        outward_weight.T, inward_bias.reshape(hidden_units, 1),
        layer_scale.reshape(channels, 1),
    )


def per_device(
    state_field,
    cotangent,
    ocean_mask,
    kernel,
    inward_weight,
    inward_bias,
    outward_weight,
    layer_scale,
):
    channels, lat_cells, lon_cells = state_field.shape
    factor = 1.0 / math.sqrt(lat_cells * lon_cells)
    padded = extend(state_field)
    conv_out = depthwise(padded, kernel, False)
    cells = lat_cells * lon_cells
    flat_conv = conv_out.reshape(channels, cells)
    flat_field = state_field.reshape(channels, cells)
    flat_cot = cotangent.reshape(channels, cells)
    mask_float = ocean_mask.astype(jnp.float32)
    flat_mask = mask_float.reshape(1, cells)
    out_flat, grad_flat, acc_in, acc_out = fused_mlp(
        flat_conv, flat_field, flat_cot, flat_mask,
        inward_weight, inward_bias, outward_weight, layer_scale,
    )
    output_field = out_flat.reshape(channels, lat_cells, lon_cells)
    conv_grad = grad_flat.reshape(channels, lat_cells, lon_cells)
    kernel_local = kernel_terms(conv_grad, padded) * factor
    parts = (acc_in * factor, acc_out * factor, kernel_local)
    flat = jnp.concatenate([part.reshape(-1) for part in parts])
    total = flat.shape[0]
    padded_total = -(-total // 4096) * 4096
    flat = jnp.pad(flat, (0, padded_total - total))
    flat = butterfly_sum(flat, BUTTERFLY_BITS)
    sums = []
    start = 0
    for part in parts:
        sums.append(flat[start : start + part.size].reshape(part.shape))
        start += part.size
    inward_grad, outward_grad, kernel_grad = sums
    grad_padded = extend(conv_grad)
    masked_grad = mask_float[None, :, :] * cotangent.astype(jnp.float32)
    field_grad = (masked_grad + depthwise(grad_padded, kernel, True)).astype(jnp.bfloat16)
    return (output_field, field_grad, kernel_grad, inward_grad, outward_grad)


def solution(mesh):
    in_specs = (P(None, "gy", "gx"), P(None, "gy", "gx"), P("gy", "gx"), P(), P(), P(), P(), P())
    out_specs = (P(None, "gy", "gx"), P(None, "gy", "gx"), P(), P(), P())
    return jax.shard_map(
        per_device, mesh=mesh, in_specs=in_specs, out_specs=out_specs, check_vma=False
    )
```

```python
import math

import jax
import jax.numpy as jnp
from jax import lax
from jax.sharding import PartitionSpec as P
from jax.experimental import pallas as pl
from jax.experimental.pallas import tpu as pltpu


def padded_2(block, sides, width, periodic):
    for axis, dim in sides:
        count = lax.axis_size(axis)
        forward = [(i, i + 1) for i in range(count - 1)]
        if periodic:
            forward.append((count - 1, 0))
        backward = [(target, source) for source, target in forward]
        low = lax.ppermute(
            lax.slice_in_dim(block, block.shape[dim] - width, None, axis=dim), axis, forward
        )
        high = lax.ppermute(lax.slice_in_dim(block, 0, width, axis=dim), axis, backward)
        block = jnp.concatenate([low, block, high], axis=dim)
    return block


BUTTERFLY_STEPS = (
    ("gx", 0), ("gy", 0), ("gx", 1), ("gx", 2), ("gy", 1), ("gx", 3), ("gy", 2), ("gy", 3)
)


def butterfly_sum(flat, steps):
    trail = []
    for axis, bit in steps:
        if 1 << bit >= lax.axis_size(axis):
            continue
        count = lax.axis_size(axis)
        mine = (lax.axis_index(axis) >> bit) & 1
        pairs = [(i, i ^ (1 << bit)) for i in range(count)]
        half = flat.shape[0] // 2
        low, high = flat[:half], flat[half:]
        sent = jnp.where(mine == 0, high, low)
        kept = jnp.where(mine == 0, low, high)
        flat = kept + lax.ppermute(sent, axis, pairs)
        trail.append((axis, mine, pairs))
    for axis, mine, pairs in reversed(trail):
        other = lax.ppermute(flat, axis, pairs)
        flat = jnp.where(
            mine == 0, jnp.concatenate([flat, other]), jnp.concatenate([other, flat])
        )
    return flat


def gelu_value(values):
    return 0.5 * values * (1.0 + jax.scipy.special.erf(values / math.sqrt(2.0)))


def gelu_slope(values):
    return 0.5 * (1.0 + jax.scipy.special.erf(values / math.sqrt(2.0))) + values * jnp.exp(
        -0.5 * values * values
    ) / math.sqrt(2.0 * math.pi)


def extend(source):
    lat_cells = source.shape[1]
    wrapped = padded_2(source, (("gx", 2),), 3, True)
    extended = padded_2(wrapped, (("gy", 1),), 3, False)
    top_strip = wrapped[:, lat_cells - 3 :, :]
    count = lax.axis_size("gx")
    facing = lax.ppermute(top_strip, "gx", [(i, count - 1 - i) for i in range(count)])
    folded = jnp.flip(facing, (1, 2))
    at_top = lax.axis_index("gy") == lax.axis_size("gy") - 1
    upper_rows = jnp.where(at_top, folded, extended[:, lat_cells + 3 :, :])
    return jnp.concatenate([extended[:, : lat_cells + 3, :], upper_rows], axis=1)


def depthwise(padded, kernel, flipped):
    lat_cells = padded.shape[1] - 6
    lon_cells = padded.shape[2] - 6
    summed = jnp.zeros((padded.shape[0], lat_cells, lon_cells), jnp.float32)
    for row_tap in range(7):
        for col_tap in range(7):
            if flipped:
                weights = kernel[:, 6 - row_tap, 6 - col_tap]
            else:
                weights = kernel[:, row_tap, col_tap]
            window = padded[:, row_tap : row_tap + lat_cells, col_tap : col_tap + lon_cells].astype(
                jnp.float32
            )
            summed = summed + weights[:, None, None] * window
    return summed


def kernel_terms(grad_half, padded):
    lat_cells = grad_half.shape[1]
    lon_cells = grad_half.shape[2]
    padded_rows = padded.shape[1]
    taps = padded_rows - lat_cells + 1
    shifted = jnp.stack(
        [padded[:, :, col_tap : col_tap + lon_cells] for col_tap in range(taps)], axis=0
    )
    by_row = jnp.einsum(
        "bcpj,cij->bcpi", shifted, grad_half, preferred_element_type=jnp.float32
    )
    diagonal = (
        jnp.arange(padded_rows)[None, :, None]
        == jnp.arange(lat_cells)[None, None, :] + jnp.arange(taps)[:, None, None]
    ).astype(jnp.float32)
    return jnp.einsum(
        "bcpi,api->cab", by_row, diagonal, precision=lax.Precision.HIGHEST,
        preferred_element_type=jnp.float32,
    )


TILE = 512


def mlp_kernel(
    conv_ref, field_ref, cot_ref, mask_ref, win_t_ref, win_ref, wout_ref, wout_t_ref,
    bias_ref, scale_ref, out_ref, grad_ref, acc_in_ref, acc_out_ref,
):
    @pl.when(pl.program_id(0) == 0)
    def _():
        acc_in_ref[...] = jnp.zeros_like(acc_in_ref)
        acc_out_ref[...] = jnp.zeros_like(acc_out_ref)

    conv = conv_ref[...]
    channels = conv.shape[0]
    average = jnp.sum(conv, axis=0, keepdims=True) / channels
    centered = conv - average
    variance = jnp.sum(centered * centered, axis=0, keepdims=True) / channels
    inverse = lax.rsqrt(variance + 1e-06)
    normed = centered * inverse
    normed_half = normed.astype(jnp.bfloat16)
    pre_act = jnp.dot(win_t_ref[...], normed_half, preferred_element_type=jnp.float32)
    pre_act = pre_act + bias_ref[...]
    hidden = gelu_value(pre_act).astype(jnp.bfloat16)
    branch = jnp.dot(wout_t_ref[...], hidden, preferred_element_type=jnp.float32)
    mask = mask_ref[...]
    scale = scale_ref[...]
    out_ref[...] = (
        mask * (field_ref[...].astype(jnp.float32) + scale * branch)
    ).astype(out_ref.dtype)
    masked_grad = mask * cot_ref[...].astype(jnp.float32)
    branch_grad = (scale * masked_grad).astype(jnp.bfloat16)
    rows_contract = (((1,), (1,)), ((), ()))
    acc_out_ref[...] += lax.dot_general(
        hidden, branch_grad, rows_contract, preferred_element_type=jnp.float32
    )
    hidden_grad = jnp.dot(wout_ref[...], branch_grad, preferred_element_type=jnp.float32)
    pre_grad = (hidden_grad * gelu_slope(pre_act)).astype(jnp.bfloat16)
    acc_in_ref[...] += lax.dot_general(
        normed_half, pre_grad, rows_contract, preferred_element_type=jnp.float32
    )
    normed_grad = jnp.dot(win_ref[...], pre_grad, preferred_element_type=jnp.float32)
    mean_grad = jnp.sum(normed_grad, axis=0, keepdims=True) / channels
    mean_prod = jnp.sum(normed_grad * normed, axis=0, keepdims=True) / channels
    grad_ref[...] = (inverse * (normed_grad - mean_grad - normed * mean_prod)).astype(
        grad_ref.dtype
    )


def fused_mlp(conv, field, cot, mask, inward_weight, inward_bias, outward_weight, layer_scale):
    channels, cells = conv.shape
    hidden_units = inward_weight.shape[1]
    tile = TILE if cells % TILE == 0 else cells
    steps = cells // tile
    cell_block = lambda rows: pl.BlockSpec((rows, tile), lambda i: (0, i))
    whole = lambda shape: pl.BlockSpec(shape, lambda i: (0, 0))
    flops = 2 * 6 * channels * hidden_units * cells
    return pl.pallas_call(
        mlp_kernel,
        grid=(steps,),
        in_specs=[
            cell_block(channels), cell_block(channels), cell_block(channels), cell_block(1),
            whole((hidden_units, channels)), whole((channels, hidden_units)),
            whole((hidden_units, channels)), whole((channels, hidden_units)),
            whole((hidden_units, 1)), whole((channels, 1)),
        ],
        out_specs=[
            cell_block(channels), cell_block(channels),
            whole((channels, hidden_units)), whole((hidden_units, channels)),
        ],
        out_shape=[
            jax.ShapeDtypeStruct((channels, cells), jnp.bfloat16),
            jax.ShapeDtypeStruct((channels, cells), jnp.bfloat16),
            jax.ShapeDtypeStruct((channels, hidden_units), jnp.float32),
            jax.ShapeDtypeStruct((hidden_units, channels), jnp.float32),
        ],
        compiler_params=pltpu.CompilerParams(dimension_semantics=("arbitrary",)),
        cost_estimate=pl.CostEstimate(
            flops=flops, transcendentals=3 * hidden_units * cells,
            bytes_accessed=channels * cells * 12,
        ),
    )(
        conv, field, cot, mask, inward_weight.T, inward_weight, outward_weight,
        outward_weight.T, inward_bias.reshape(hidden_units, 1),
        layer_scale.reshape(channels, 1),
    )


def per_device(
    state_field,
    cotangent,
    ocean_mask,
    kernel,
    inward_weight,
    inward_bias,
    outward_weight,
    layer_scale,
):
    channels, lat_cells, lon_cells = state_field.shape
    factor = 1.0 / math.sqrt(lat_cells * lon_cells)
    padded = extend(state_field)
    conv_out = depthwise(padded, kernel, False)
    cells = lat_cells * lon_cells
    flat_conv = conv_out.reshape(channels, cells)
    flat_field = state_field.reshape(channels, cells)
    flat_cot = cotangent.reshape(channels, cells)
    mask_float = ocean_mask.astype(jnp.float32)
    flat_mask = mask_float.reshape(1, cells)
    out_flat, grad_flat, acc_in, acc_out = fused_mlp(
        flat_conv, flat_field, flat_cot, flat_mask,
        inward_weight, inward_bias, outward_weight, layer_scale,
    )
    output_field = out_flat.reshape(channels, lat_cells, lon_cells)
    conv_grad = grad_flat.reshape(channels, lat_cells, lon_cells)
    kernel_local = kernel_terms(conv_grad, padded) * factor
    parts = (acc_in * factor, acc_out * factor, kernel_local)
    flat = jnp.concatenate([part.reshape(-1) for part in parts])
    total = flat.shape[0]
    padded_total = -(-total // 2048) * 2048
    flat = jnp.pad(flat, (0, padded_total - total))
    flat = butterfly_sum(flat, BUTTERFLY_STEPS)
    sums = []
    start = 0
    for part in parts:
        sums.append(flat[start : start + part.size].reshape(part.shape))
        start += part.size
    inward_grad, outward_grad, kernel_grad = sums
    grad_padded = extend(conv_grad)
    masked_grad = mask_float[None, :, :] * cotangent.astype(jnp.float32)
    field_grad = (masked_grad + depthwise(grad_padded, kernel, True)).astype(jnp.bfloat16)
    return (output_field, field_grad, kernel_grad, inward_grad, outward_grad)


def solution(mesh):
    in_specs = (P(None, "gy", "gx"), P(None, "gy", "gx"), P("gy", "gx"), P(), P(), P(), P(), P())
    out_specs = (P(None, "gy", "gx"), P(None, "gy", "gx"), P(), P(), P())
    return jax.shard_map(
        per_device, mesh=mesh, in_specs=in_specs, out_specs=out_specs, check_vma=False
    )
```

```python
import math

import jax
import jax.numpy as jnp
from jax import lax
from jax.sharding import PartitionSpec as P
from jax.experimental import pallas as pl
from jax.experimental.pallas import tpu as pltpu


def padded_2(block, sides, width, periodic):
    for axis, dim in sides:
        count = lax.axis_size(axis)
        forward = [(i, i + 1) for i in range(count - 1)]
        if periodic:
            forward.append((count - 1, 0))
        backward = [(target, source) for source, target in forward]
        low = lax.ppermute(
            lax.slice_in_dim(block, block.shape[dim] - width, None, axis=dim), axis, forward
        )
        high = lax.ppermute(lax.slice_in_dim(block, 0, width, axis=dim), axis, backward)
        block = jnp.concatenate([low, block, high], axis=dim)
    return block


BUTTERFLY_STEPS = (
    ("gx", 0), ("gy", 0), ("gx", 1), ("gx", 2), ("gy", 1), ("gx", 3), ("gy", 2), ("gy", 3)
)


def butterfly_sum(flat, steps, late=None):
    trail = []
    for axis, bit in steps:
        if 1 << bit >= lax.axis_size(axis):
            continue
        count = lax.axis_size(axis)
        mine = (lax.axis_index(axis) >> bit) & 1
        pairs = [(i, i ^ (1 << bit)) for i in range(count)]
        half = flat.shape[0] // 2
        low, high = flat[:half], flat[half:]
        sent = jnp.where(mine == 0, high, low)
        kept = jnp.where(mine == 0, low, high)
        flat = kept + lax.ppermute(sent, axis, pairs)
        trail.append((axis, mine, pairs))
    extra = late()
    for axis, mine, pairs in reversed(trail):
        size = flat.shape[0]
        got = lax.ppermute(jnp.concatenate([flat, extra]), axis, pairs)
        other = got[:size]
        extra = extra + got[size:]
        flat = jnp.where(
            mine == 0, jnp.concatenate([flat, other]), jnp.concatenate([other, flat])
        )
    return flat, extra


def gelu_value(values):
    return 0.5 * values * (1.0 + jax.scipy.special.erf(values / math.sqrt(2.0)))


def gelu_slope(values):
    return 0.5 * (1.0 + jax.scipy.special.erf(values / math.sqrt(2.0))) + values * jnp.exp(
        -0.5 * values * values
    ) / math.sqrt(2.0 * math.pi)


def extend(source):
    lat_cells = source.shape[1]
    wrapped = padded_2(source, (("gx", 2),), 3, True)
    extended = padded_2(wrapped, (("gy", 1),), 3, False)
    top_strip = wrapped[:, lat_cells - 3 :, :]
    count = lax.axis_size("gx")
    facing = lax.ppermute(top_strip, "gx", [(i, count - 1 - i) for i in range(count)])
    folded = jnp.flip(facing, (1, 2))
    at_top = lax.axis_index("gy") == lax.axis_size("gy") - 1
    upper_rows = jnp.where(at_top, folded, extended[:, lat_cells + 3 :, :])
    return jnp.concatenate([extended[:, : lat_cells + 3, :], upper_rows], axis=1)


def depthwise(padded, kernel, flipped):
    lat_cells = padded.shape[1] - 6
    lon_cells = padded.shape[2] - 6
    summed = jnp.zeros((padded.shape[0], lat_cells, lon_cells), jnp.float32)
    for row_tap in range(7):
        for col_tap in range(7):
            if flipped:
                weights = kernel[:, 6 - row_tap, 6 - col_tap]
            else:
                weights = kernel[:, row_tap, col_tap]
            window = padded[:, row_tap : row_tap + lat_cells, col_tap : col_tap + lon_cells].astype(
                jnp.float32
            )
            summed = summed + weights[:, None, None] * window
    return summed


def KTERM_SPLIT(row_taps):
    return (tuple(range(0, 3)), tuple(range(3, 5)), tuple(range(5, row_taps)))


def kernel_terms(grad_half, padded, row_taps):
    lat_cells = grad_half.shape[1]
    lon_cells = grad_half.shape[2]
    grad_float = grad_half.astype(jnp.float32)
    row_sums = []
    for row_tap in row_taps:
        column_sums = []
        for col_tap in range(7):
            window = padded[:, row_tap : row_tap + lat_cells, col_tap : col_tap + lon_cells].astype(
                jnp.float32
            )
            column_sums.append(jnp.sum(grad_float * window, axis=(1, 2)))
        row_sums.append(jnp.stack(column_sums, axis=1))
    return jnp.stack(row_sums, axis=1)


TILE = 512


def mlp_kernel(
    conv_ref, field_ref, cot_ref, mask_ref, win_t_ref, win_ref, wout_ref, wout_t_ref,
    bias_ref, scale_ref, out_ref, grad_ref, acc_in_ref, acc_out_ref,
):
    @pl.when(pl.program_id(0) == 0)
    def _():
        acc_in_ref[...] = jnp.zeros_like(acc_in_ref)
        acc_out_ref[...] = jnp.zeros_like(acc_out_ref)

    conv = conv_ref[...]
    channels = conv.shape[0]
    average = jnp.sum(conv, axis=0, keepdims=True) / channels
    centered = conv - average
    variance = jnp.sum(centered * centered, axis=0, keepdims=True) / channels
    inverse = lax.rsqrt(variance + 1e-06)
    normed = centered * inverse
    normed_half = normed.astype(jnp.bfloat16)
    pre_act = jnp.dot(win_t_ref[...], normed_half, preferred_element_type=jnp.float32)
    pre_act = pre_act + bias_ref[...]
    hidden = gelu_value(pre_act).astype(jnp.bfloat16)
    branch = jnp.dot(wout_t_ref[...], hidden, preferred_element_type=jnp.float32)
    mask = mask_ref[...]
    scale = scale_ref[...]
    out_ref[...] = (
        mask * (field_ref[...].astype(jnp.float32) + scale * branch)
    ).astype(out_ref.dtype)
    masked_grad = mask * cot_ref[...].astype(jnp.float32)
    branch_grad = (scale * masked_grad).astype(jnp.bfloat16)
    rows_contract = (((1,), (1,)), ((), ()))
    acc_out_ref[...] += lax.dot_general(
        hidden, branch_grad, rows_contract, preferred_element_type=jnp.float32
    )
    hidden_grad = jnp.dot(wout_ref[...], branch_grad, preferred_element_type=jnp.float32)
    pre_grad = (hidden_grad * gelu_slope(pre_act)).astype(jnp.bfloat16)
    acc_in_ref[...] += lax.dot_general(
        normed_half, pre_grad, rows_contract, preferred_element_type=jnp.float32
    )
    normed_grad = jnp.dot(win_ref[...], pre_grad, preferred_element_type=jnp.float32)
    mean_grad = jnp.sum(normed_grad, axis=0, keepdims=True) / channels
    mean_prod = jnp.sum(normed_grad * normed, axis=0, keepdims=True) / channels
    grad_ref[...] = (inverse * (normed_grad - mean_grad - normed * mean_prod)).astype(
        grad_ref.dtype
    )


def fused_mlp(conv, field, cot, mask, inward_weight, inward_bias, outward_weight, layer_scale):
    channels, cells = conv.shape
    hidden_units = inward_weight.shape[1]
    tile = TILE if cells % TILE == 0 else cells
    steps = cells // tile
    cell_block = lambda rows: pl.BlockSpec((rows, tile), lambda i: (0, i))
    whole = lambda shape: pl.BlockSpec(shape, lambda i: (0, 0))
    flops = 2 * 6 * channels * hidden_units * cells
    return pl.pallas_call(
        mlp_kernel,
        grid=(steps,),
        in_specs=[
            cell_block(channels), cell_block(channels), cell_block(channels), cell_block(1),
            whole((hidden_units, channels)), whole((channels, hidden_units)),
            whole((hidden_units, channels)), whole((channels, hidden_units)),
            whole((hidden_units, 1)), whole((channels, 1)),
        ],
        out_specs=[
            cell_block(channels), cell_block(channels),
            whole((channels, hidden_units)), whole((hidden_units, channels)),
        ],
        out_shape=[
            jax.ShapeDtypeStruct((channels, cells), jnp.bfloat16),
            jax.ShapeDtypeStruct((channels, cells), jnp.bfloat16),
            jax.ShapeDtypeStruct((channels, hidden_units), jnp.float32),
            jax.ShapeDtypeStruct((hidden_units, channels), jnp.float32),
        ],
        compiler_params=pltpu.CompilerParams(dimension_semantics=("arbitrary",)),
        cost_estimate=pl.CostEstimate(
            flops=flops, transcendentals=3 * hidden_units * cells,
            bytes_accessed=channels * cells * 12,
        ),
    )(
        conv, field, cot, mask, inward_weight.T, inward_weight, outward_weight,
        outward_weight.T, inward_bias.reshape(hidden_units, 1),
        layer_scale.reshape(channels, 1),
    )


def per_device(
    state_field,
    cotangent,
    ocean_mask,
    kernel,
    inward_weight,
    inward_bias,
    outward_weight,
    layer_scale,
):
    channels, lat_cells, lon_cells = state_field.shape
    factor = 1.0 / math.sqrt(lat_cells * lon_cells)
    padded = extend(state_field)
    conv_out = depthwise(padded, kernel, False)
    cells = lat_cells * lon_cells
    flat_conv = conv_out.reshape(channels, cells)
    flat_field = state_field.reshape(channels, cells)
    flat_cot = cotangent.reshape(channels, cells)
    mask_float = ocean_mask.astype(jnp.float32)
    flat_mask = mask_float.reshape(1, cells)
    out_flat, grad_flat, acc_in, acc_out = fused_mlp(
        flat_conv, flat_field, flat_cot, flat_mask,
        inward_weight, inward_bias, outward_weight, layer_scale,
    )
    output_field = out_flat.reshape(channels, lat_cells, lon_cells)
    conv_grad = grad_flat.reshape(channels, lat_cells, lon_cells)
    parts = (acc_in * factor, acc_out * factor)
    flat = jnp.concatenate([part.reshape(-1) for part in parts])
    total = flat.shape[0]
    padded_total = -(-total // 2048) * 2048
    flat = jnp.pad(flat, (0, padded_total - total))

    def kernel_part():
        row_taps = padded.shape[1] - lat_cells + 1
        pieces = []
        for taps in KTERM_SPLIT(row_taps):
            pieces.append(kernel_terms(conv_grad, padded, taps) * factor)
        return jnp.concatenate(pieces, axis=1).reshape(-1)

    flat, kernel_flat = butterfly_sum(flat, BUTTERFLY_STEPS, kernel_part)
    sums = []
    start = 0
    for part in parts:
        sums.append(flat[start : start + part.size].reshape(part.shape))
        start += part.size
    sums.append(kernel_flat.reshape(channels, 7, 7))
    inward_grad, outward_grad, kernel_grad = sums
    grad_padded = extend(conv_grad)
    masked_grad = mask_float[None, :, :] * cotangent.astype(jnp.float32)
    field_grad = (masked_grad + depthwise(grad_padded, kernel, True)).astype(jnp.bfloat16)
    return (output_field, field_grad, kernel_grad, inward_grad, outward_grad)


def solution(mesh):
    in_specs = (P(None, "gy", "gx"), P(None, "gy", "gx"), P("gy", "gx"), P(), P(), P(), P(), P())
    out_specs = (P(None, "gy", "gx"), P(None, "gy", "gx"), P(), P(), P())
    return jax.shard_map(
        per_device, mesh=mesh, in_specs=in_specs, out_specs=out_specs, check_vma=False
    )
```

```python
import math

import jax
import jax.numpy as jnp
from jax import lax
from jax.sharding import PartitionSpec as P
from jax.experimental import pallas as pl
from jax.experimental.pallas import tpu as pltpu


def padded_2(block, sides, width, periodic):
    for axis, dim in sides:
        count = lax.axis_size(axis)
        forward = [(i, i + 1) for i in range(count - 1)]
        if periodic:
            forward.append((count - 1, 0))
        backward = [(target, source) for source, target in forward]
        low = lax.ppermute(
            lax.slice_in_dim(block, block.shape[dim] - width, None, axis=dim), axis, forward
        )
        high = lax.ppermute(lax.slice_in_dim(block, 0, width, axis=dim), axis, backward)
        block = jnp.concatenate([low, block, high], axis=dim)
    return block


def from_partner(block, axis, distance):
    count = lax.axis_size(axis)
    route = []
    for low in range(count):
        high = low | 1 << distance
        if high != low and high < count:
            route += [(low, high), (high, low)]
    return lax.ppermute(block, axis, route)


BUTTERFLY_STEPS = (
    ("gx", 0), ("gy", 0), ("gx", 1), ("gx", 2), ("gy", 1), ("gx", 3), ("gy", 2), ("gy", 3)
)


def butterfly_sum(flat, steps):
    trail = []
    for axis, bit in steps:
        if 1 << bit >= lax.axis_size(axis):
            continue
        count = lax.axis_size(axis)
        mine = (lax.axis_index(axis) >> bit) & 1
        pairs = [(i, i ^ (1 << bit)) for i in range(count)]
        half = flat.shape[0] // 2
        low, high = flat[:half], flat[half:]
        sent = jnp.where(mine == 0, high, low)
        kept = jnp.where(mine == 0, low, high)
        flat = kept + lax.ppermute(sent, axis, pairs)
        trail.append((axis, mine, pairs))
    for axis, mine, pairs in reversed(trail):
        other = lax.ppermute(flat, axis, pairs)
        flat = jnp.where(
            mine == 0, jnp.concatenate([flat, other]), jnp.concatenate([other, flat])
        )
    return flat


def gelu_value(values):
    return 0.5 * values * (1.0 + jax.scipy.special.erf(values / math.sqrt(2.0)))


def gelu_slope(values):
    return 0.5 * (1.0 + jax.scipy.special.erf(values / math.sqrt(2.0))) + values * jnp.exp(
        -0.5 * values * values
    ) / math.sqrt(2.0 * math.pi)


def extend(source):
    lat_cells = source.shape[1]
    wrapped = padded_2(source, (("gx", 2),), 3, True)
    extended = padded_2(wrapped, (("gy", 1),), 3, False)
    top_strip = wrapped[:, lat_cells - 3 :, :]
    count = lax.axis_size("gx")
    facing = lax.ppermute(top_strip, "gx", [(i, count - 1 - i) for i in range(count)])
    folded = jnp.flip(facing, (1, 2))
    at_top = lax.axis_index("gy") == lax.axis_size("gy") - 1
    upper_rows = jnp.where(at_top, folded, extended[:, lat_cells + 3 :, :])
    return jnp.concatenate([extended[:, : lat_cells + 3, :], upper_rows], axis=1)


def depthwise(padded, kernel, flipped):
    lat_cells = padded.shape[1] - 6
    lon_cells = padded.shape[2] - 6
    summed = jnp.zeros((padded.shape[0], lat_cells, lon_cells), jnp.float32)
    for row_tap in range(7):
        for col_tap in range(7):
            if flipped:
                weights = kernel[:, 6 - row_tap, 6 - col_tap]
            else:
                weights = kernel[:, row_tap, col_tap]
            window = padded[:, row_tap : row_tap + lat_cells, col_tap : col_tap + lon_cells].astype(
                jnp.float32
            )
            summed = summed + weights[:, None, None] * window
    return summed


def kernel_terms(grad_half, padded):
    lat_cells = grad_half.shape[1]
    lon_cells = grad_half.shape[2]
    grad_float = grad_half.astype(jnp.float32)
    row_sums = []
    for row_tap in range(7):
        column_sums = []
        for col_tap in range(7):
            window = padded[:, row_tap : row_tap + lat_cells, col_tap : col_tap + lon_cells].astype(
                jnp.float32
            )
            column_sums.append(jnp.sum(grad_float * window, axis=1))
        row_sums.append(jnp.stack(column_sums, axis=1))
    return jnp.sum(jnp.stack(row_sums, axis=1), axis=-1)


def mlp_block(
    conv_out, field_blk, cot_blk, mask_blk, inward_weight, inward_bias, outward_weight, layer_scale
):
    average = jnp.mean(conv_out, axis=0, keepdims=True)
    centered = conv_out - average
    variance = jnp.mean(centered * centered, axis=0, keepdims=True)
    inverse = lax.rsqrt(variance + 1e-06)
    normed = centered * inverse
    normed_half = normed.astype(jnp.bfloat16)
    contract = (((0,), (0,)), ((), ()))
    pre_act = (
        lax.dot_general(inward_weight, normed_half, contract, preferred_element_type=jnp.float32)
        + inward_bias[:, None]
    )
    hidden = gelu_value(pre_act).astype(jnp.bfloat16)
    branch = lax.dot_general(outward_weight, hidden, contract, preferred_element_type=jnp.float32)
    output_blk = (
        mask_blk * (field_blk.astype(jnp.float32) + layer_scale[:, None] * branch)
    ).astype(jnp.bfloat16)
    masked_grad = mask_blk * cot_blk.astype(jnp.float32)
    branch_grad = (layer_scale[:, None] * masked_grad).astype(jnp.bfloat16)
    rows_contract = (((1,), (1,)), ((), ()))
    outward_part = lax.dot_general(
        hidden, branch_grad, rows_contract, preferred_element_type=jnp.float32
    )
    hidden_grad = jnp.dot(outward_weight, branch_grad, preferred_element_type=jnp.float32)
    pre_grad = (hidden_grad * gelu_slope(pre_act)).astype(jnp.bfloat16)
    inward_part = lax.dot_general(
        normed_half, pre_grad, rows_contract, preferred_element_type=jnp.float32
    )
    normed_grad = jnp.dot(inward_weight, pre_grad, preferred_element_type=jnp.float32)
    mean_grad = jnp.mean(normed_grad, axis=0, keepdims=True)
    mean_prod = jnp.mean(normed_grad * normed, axis=0, keepdims=True)
    conv_grad = (inverse * (normed_grad - mean_grad - normed * mean_prod)).astype(jnp.bfloat16)
    return (output_blk, conv_grad, inward_part, outward_part)


TILE = 512


def mlp_kernel(
    conv_ref, field_ref, cot_ref, mask_ref, win_t_ref, win_ref, wout_ref, wout_t_ref,
    bias_ref, scale_ref, out_ref, grad_ref, acc_in_ref, acc_out_ref,
):
    @pl.when(pl.program_id(0) == 0)
    def _():
        acc_in_ref[...] = jnp.zeros_like(acc_in_ref)
        acc_out_ref[...] = jnp.zeros_like(acc_out_ref)

    conv = conv_ref[...]
    channels = conv.shape[0]
    average = jnp.sum(conv, axis=0, keepdims=True) / channels
    centered = conv - average
    variance = jnp.sum(centered * centered, axis=0, keepdims=True) / channels
    inverse = lax.rsqrt(variance + 1e-06)
    normed = centered * inverse
    normed_half = normed.astype(jnp.bfloat16)
    pre_act = jnp.dot(win_t_ref[...], normed_half, preferred_element_type=jnp.float32)
    pre_act = pre_act + bias_ref[...]
    hidden = gelu_value(pre_act).astype(jnp.bfloat16)
    branch = jnp.dot(wout_t_ref[...], hidden, preferred_element_type=jnp.float32)
    mask = mask_ref[...]
    scale = scale_ref[...]
    out_ref[...] = (
        mask * (field_ref[...].astype(jnp.float32) + scale * branch)
    ).astype(out_ref.dtype)
    masked_grad = mask * cot_ref[...].astype(jnp.float32)
    branch_grad = (scale * masked_grad).astype(jnp.bfloat16)
    rows_contract = (((1,), (1,)), ((), ()))
    acc_out_ref[...] += lax.dot_general(
        hidden, branch_grad, rows_contract, preferred_element_type=jnp.float32
    )
    hidden_grad = jnp.dot(wout_ref[...], branch_grad, preferred_element_type=jnp.float32)
    pre_grad = (hidden_grad * gelu_slope(pre_act)).astype(jnp.bfloat16)
    acc_in_ref[...] += lax.dot_general(
        normed_half, pre_grad, rows_contract, preferred_element_type=jnp.float32
    )
    normed_grad = jnp.dot(win_ref[...], pre_grad, preferred_element_type=jnp.float32)
    mean_grad = jnp.sum(normed_grad, axis=0, keepdims=True) / channels
    mean_prod = jnp.sum(normed_grad * normed, axis=0, keepdims=True) / channels
    grad_ref[...] = (inverse * (normed_grad - mean_grad - normed * mean_prod)).astype(
        grad_ref.dtype
    )


def fused_mlp(conv, field, cot, mask, inward_weight, inward_bias, outward_weight, layer_scale):
    channels, cells = conv.shape
    hidden_units = inward_weight.shape[1]
    tile = TILE if cells % TILE == 0 else cells
    steps = cells // tile
    cell_block = lambda rows: pl.BlockSpec((rows, tile), lambda i: (0, i))
    whole = lambda shape: pl.BlockSpec(shape, lambda i: (0, 0))
    flops = 2 * 6 * channels * hidden_units * cells
    return pl.pallas_call(
        mlp_kernel,
        grid=(steps,),
        in_specs=[
            cell_block(channels), cell_block(channels), cell_block(channels), cell_block(1),
            whole((hidden_units, channels)), whole((channels, hidden_units)),
            whole((hidden_units, channels)), whole((channels, hidden_units)),
            whole((hidden_units, 1)), whole((channels, 1)),
        ],
        out_specs=[
            cell_block(channels), cell_block(channels),
            whole((channels, hidden_units)), whole((hidden_units, channels)),
        ],
        out_shape=[
            jax.ShapeDtypeStruct((channels, cells), jnp.bfloat16),
            jax.ShapeDtypeStruct((channels, cells), jnp.bfloat16),
            jax.ShapeDtypeStruct((channels, hidden_units), jnp.float32),
            jax.ShapeDtypeStruct((hidden_units, channels), jnp.float32),
        ],
        compiler_params=pltpu.CompilerParams(dimension_semantics=("arbitrary",)),
        cost_estimate=pl.CostEstimate(
            flops=flops, transcendentals=3 * hidden_units * cells,
            bytes_accessed=channels * cells * 12,
        ),
    )(
        conv, field, cot, mask, inward_weight.T, inward_weight, outward_weight,
        outward_weight.T, inward_bias.reshape(hidden_units, 1),
        layer_scale.reshape(channels, 1),
    )


def per_device(
    state_field,
    cotangent,
    ocean_mask,
    kernel,
    inward_weight,
    inward_bias,
    outward_weight,
    layer_scale,
):
    channels, lat_cells, lon_cells = state_field.shape
    hidden_units = inward_weight.shape[1]
    factor = 1.0 / math.sqrt(lat_cells * lon_cells)
    padded = extend(state_field)
    conv_out = depthwise(padded, kernel, False)
    cells = lat_cells * lon_cells
    flat_conv = conv_out.reshape(channels, cells)
    flat_field = state_field.reshape(channels, cells)
    flat_cot = cotangent.reshape(channels, cells)
    mask_float = ocean_mask.astype(jnp.float32)
    flat_mask = mask_float.reshape(1, cells)
    out_flat, grad_flat, acc_in, acc_out = fused_mlp(
        flat_conv, flat_field, flat_cot, flat_mask,
        inward_weight, inward_bias, outward_weight, layer_scale,
    )
    output_field = out_flat.reshape(channels, lat_cells, lon_cells)
    conv_grad = grad_flat.reshape(channels, lat_cells, lon_cells)
    kernel_local = kernel_terms(conv_grad, padded) * factor
    parts = (acc_in * factor, acc_out * factor, kernel_local)
    flat = jnp.concatenate([part.reshape(-1) for part in parts])
    total = flat.shape[0]
    padded_total = -(-total // 2048) * 2048
    flat = jnp.pad(flat, (0, padded_total - total))
    flat = butterfly_sum(flat, BUTTERFLY_STEPS)
    sums = []
    start = 0
    for part in parts:
        sums.append(flat[start : start + part.size].reshape(part.shape))
        start += part.size
    inward_grad, outward_grad, kernel_grad = sums
    grad_padded = extend(conv_grad)
    masked_grad = mask_float[None, :, :] * cotangent.astype(jnp.float32)
    field_grad = (masked_grad + depthwise(grad_padded, kernel, True)).astype(jnp.bfloat16)
    return (output_field, field_grad, kernel_grad, inward_grad, outward_grad)


def solution(mesh):
    in_specs = (P(None, "gy", "gx"), P(None, "gy", "gx"), P("gy", "gx"), P(), P(), P(), P(), P())
    out_specs = (P(None, "gy", "gx"), P(None, "gy", "gx"), P(), P(), P())
    return jax.shard_map(
        per_device, mesh=mesh, in_specs=in_specs, out_specs=out_specs, check_vma=False
    )
```

```python
import math

import jax
import jax.numpy as jnp
from jax import lax
from jax.sharding import PartitionSpec as P
from jax.experimental import pallas as pl
from jax.experimental.pallas import tpu as pltpu


def padded_2(block, sides, width, periodic):
    for axis, dim in sides:
        count = lax.axis_size(axis)
        forward = [(i, i + 1) for i in range(count - 1)]
        if periodic:
            forward.append((count - 1, 0))
        backward = [(target, source) for source, target in forward]
        low = lax.ppermute(
            lax.slice_in_dim(block, block.shape[dim] - width, None, axis=dim), axis, forward
        )
        high = lax.ppermute(lax.slice_in_dim(block, 0, width, axis=dim), axis, backward)
        block = jnp.concatenate([low, block, high], axis=dim)
    return block


def from_partner(block, axis, distance):
    count = lax.axis_size(axis)
    route = []
    for low in range(count):
        high = low | 1 << distance
        if high != low and high < count:
            route += [(low, high), (high, low)]
    return lax.ppermute(block, axis, route)


BUTTERFLY_STEPS = (
    ("gx", 0), ("gy", 0), ("gx", 1), ("gx", 2), ("gy", 1), ("gx", 3), ("gy", 2), ("gy", 3)
)


def butterfly_sum(flat, steps):
    trail = []
    for axis, bit in steps:
        if 1 << bit >= lax.axis_size(axis):
            continue
        count = lax.axis_size(axis)
        mine = (lax.axis_index(axis) >> bit) & 1
        pairs = [(i, i ^ (1 << bit)) for i in range(count)]
        half = flat.shape[0] // 2
        low, high = flat[:half], flat[half:]
        sent = jnp.where(mine == 0, high, low)
        kept = jnp.where(mine == 0, low, high)
        flat = kept + lax.ppermute(sent, axis, pairs)
        trail.append((axis, mine, pairs))
    for axis, mine, pairs in reversed(trail):
        other = lax.ppermute(flat, axis, pairs)
        flat = jnp.where(
            mine == 0, jnp.concatenate([flat, other]), jnp.concatenate([other, flat])
        )
    return flat


def gelu_value(values):
    return 0.5 * values * (1.0 + jax.scipy.special.erf(values / math.sqrt(2.0)))


def gelu_slope(values):
    return 0.5 * (1.0 + jax.scipy.special.erf(values / math.sqrt(2.0))) + values * jnp.exp(
        -0.5 * values * values
    ) / math.sqrt(2.0 * math.pi)


def extend(source):
    lat_cells = source.shape[1]
    wrapped = padded_2(source, (("gx", 2),), 3, True)
    extended = padded_2(wrapped, (("gy", 1),), 3, False)
    top_strip = wrapped[:, lat_cells - 3 :, :]
    count = lax.axis_size("gx")
    facing = lax.ppermute(top_strip, "gx", [(i, count - 1 - i) for i in range(count)])
    folded = jnp.flip(facing, (1, 2))
    at_top = lax.axis_index("gy") == lax.axis_size("gy") - 1
    upper_rows = jnp.where(at_top, folded, extended[:, lat_cells + 3 :, :])
    return jnp.concatenate([extended[:, : lat_cells + 3, :], upper_rows], axis=1)


def depthwise(padded, kernel, flipped):
    lat_cells = padded.shape[1] - 6
    lon_cells = padded.shape[2] - 6
    summed = jnp.zeros((padded.shape[0], lat_cells, lon_cells), jnp.float32)
    for row_tap in range(7):
        for col_tap in range(7):
            if flipped:
                weights = kernel[:, 6 - row_tap, 6 - col_tap]
            else:
                weights = kernel[:, row_tap, col_tap]
            window = padded[:, row_tap : row_tap + lat_cells, col_tap : col_tap + lon_cells].astype(
                jnp.float32
            )
            summed = summed + weights[:, None, None] * window
    return summed


def kernel_terms(grad_half, padded):
    lat_cells = grad_half.shape[1]
    lon_cells = grad_half.shape[2]
    grad_float = grad_half.astype(jnp.float32)
    row_sums = []
    for row_tap in range(7):
        column_sums = []
        for col_tap in range(7):
            window = padded[:, row_tap : row_tap + lat_cells, col_tap : col_tap + lon_cells].astype(
                jnp.float32
            )
            column_sums.append(jnp.sum(grad_float * window, axis=(1, 2)))
        row_sums.append(jnp.stack(column_sums, axis=1))
    return jnp.stack(row_sums, axis=1)


def mlp_block(
    conv_out, field_blk, cot_blk, mask_blk, inward_weight, inward_bias, outward_weight, layer_scale
):
    average = jnp.mean(conv_out, axis=0, keepdims=True)
    centered = conv_out - average
    variance = jnp.mean(centered * centered, axis=0, keepdims=True)
    inverse = lax.rsqrt(variance + 1e-06)
    normed = centered * inverse
    normed_half = normed.astype(jnp.bfloat16)
    contract = (((0,), (0,)), ((), ()))
    pre_act = (
        lax.dot_general(inward_weight, normed_half, contract, preferred_element_type=jnp.float32)
        + inward_bias[:, None]
    )
    hidden = gelu_value(pre_act).astype(jnp.bfloat16)
    branch = lax.dot_general(outward_weight, hidden, contract, preferred_element_type=jnp.float32)
    output_blk = (
        mask_blk * (field_blk.astype(jnp.float32) + layer_scale[:, None] * branch)
    ).astype(jnp.bfloat16)
    masked_grad = mask_blk * cot_blk.astype(jnp.float32)
    branch_grad = (layer_scale[:, None] * masked_grad).astype(jnp.bfloat16)
    rows_contract = (((1,), (1,)), ((), ()))
    outward_part = lax.dot_general(
        hidden, branch_grad, rows_contract, preferred_element_type=jnp.float32
    )
    hidden_grad = jnp.dot(outward_weight, branch_grad, preferred_element_type=jnp.float32)
    pre_grad = (hidden_grad * gelu_slope(pre_act)).astype(jnp.bfloat16)
    inward_part = lax.dot_general(
        normed_half, pre_grad, rows_contract, preferred_element_type=jnp.float32
    )
    normed_grad = jnp.dot(inward_weight, pre_grad, preferred_element_type=jnp.float32)
    mean_grad = jnp.mean(normed_grad, axis=0, keepdims=True)
    mean_prod = jnp.mean(normed_grad * normed, axis=0, keepdims=True)
    conv_grad = (inverse * (normed_grad - mean_grad - normed * mean_prod)).astype(jnp.bfloat16)
    return (output_blk, conv_grad, inward_part, outward_part)


TILE = 1024


def mlp_kernel(
    conv_ref, field_ref, cot_ref, mask_ref, win_t_ref, win_ref, wout_ref, wout_t_ref,
    bias_ref, scale_ref, out_ref, grad_ref, acc_in_ref, acc_out_ref,
):
    @pl.when(pl.program_id(0) == 0)
    def _():
        acc_in_ref[...] = jnp.zeros_like(acc_in_ref)
        acc_out_ref[...] = jnp.zeros_like(acc_out_ref)

    conv = conv_ref[...]
    channels = conv.shape[0]
    average = jnp.sum(conv, axis=0, keepdims=True) / channels
    centered = conv - average
    variance = jnp.sum(centered * centered, axis=0, keepdims=True) / channels
    inverse = lax.rsqrt(variance + 1e-06)
    normed = centered * inverse
    normed_half = normed.astype(jnp.bfloat16)
    pre_act = jnp.dot(win_t_ref[...], normed_half, preferred_element_type=jnp.float32)
    pre_act = pre_act + bias_ref[...]
    hidden = gelu_value(pre_act).astype(jnp.bfloat16)
    branch = jnp.dot(wout_t_ref[...], hidden, preferred_element_type=jnp.float32)
    mask = mask_ref[...]
    scale = scale_ref[...]
    out_ref[...] = (
        mask * (field_ref[...].astype(jnp.float32) + scale * branch)
    ).astype(out_ref.dtype)
    masked_grad = mask * cot_ref[...].astype(jnp.float32)
    branch_grad = (scale * masked_grad).astype(jnp.bfloat16)
    rows_contract = (((1,), (1,)), ((), ()))
    acc_out_ref[...] += lax.dot_general(
        hidden, branch_grad, rows_contract, preferred_element_type=jnp.float32
    )
    hidden_grad = jnp.dot(wout_ref[...], branch_grad, preferred_element_type=jnp.float32)
    pre_grad = (hidden_grad * gelu_slope(pre_act)).astype(jnp.bfloat16)
    acc_in_ref[...] += lax.dot_general(
        normed_half, pre_grad, rows_contract, preferred_element_type=jnp.float32
    )
    normed_grad = jnp.dot(win_ref[...], pre_grad, preferred_element_type=jnp.float32)
    mean_grad = jnp.sum(normed_grad, axis=0, keepdims=True) / channels
    mean_prod = jnp.sum(normed_grad * normed, axis=0, keepdims=True) / channels
    grad_ref[...] = (inverse * (normed_grad - mean_grad - normed * mean_prod)).astype(
        grad_ref.dtype
    )


def fused_mlp(conv, field, cot, mask, inward_weight, inward_bias, outward_weight, layer_scale):
    channels, cells = conv.shape
    hidden_units = inward_weight.shape[1]
    tile = TILE if cells % TILE == 0 else cells
    steps = cells // tile
    cell_block = lambda rows: pl.BlockSpec((rows, tile), lambda i: (0, i))
    whole = lambda shape: pl.BlockSpec(shape, lambda i: (0, 0))
    flops = 2 * 6 * channels * hidden_units * cells
    return pl.pallas_call(
        mlp_kernel,
        grid=(steps,),
        in_specs=[
            cell_block(channels), cell_block(channels), cell_block(channels), cell_block(1),
            whole((hidden_units, channels)), whole((channels, hidden_units)),
            whole((hidden_units, channels)), whole((channels, hidden_units)),
            whole((hidden_units, 1)), whole((channels, 1)),
        ],
        out_specs=[
            cell_block(channels), cell_block(channels),
            whole((channels, hidden_units)), whole((hidden_units, channels)),
        ],
        out_shape=[
            jax.ShapeDtypeStruct((channels, cells), jnp.bfloat16),
            jax.ShapeDtypeStruct((channels, cells), jnp.bfloat16),
            jax.ShapeDtypeStruct((channels, hidden_units), jnp.float32),
            jax.ShapeDtypeStruct((hidden_units, channels), jnp.float32),
        ],
        compiler_params=pltpu.CompilerParams(dimension_semantics=("arbitrary",)),
        cost_estimate=pl.CostEstimate(
            flops=flops, transcendentals=3 * hidden_units * cells,
            bytes_accessed=channels * cells * 12,
        ),
    )(
        conv, field, cot, mask, inward_weight.T, inward_weight, outward_weight,
        outward_weight.T, inward_bias.reshape(hidden_units, 1),
        layer_scale.reshape(channels, 1),
    )


def per_device(
    state_field,
    cotangent,
    ocean_mask,
    kernel,
    inward_weight,
    inward_bias,
    outward_weight,
    layer_scale,
):
    channels, lat_cells, lon_cells = state_field.shape
    hidden_units = inward_weight.shape[1]
    factor = 1.0 / math.sqrt(lat_cells * lon_cells)
    padded = extend(state_field)
    conv_out = depthwise(padded, kernel, False)
    cells = lat_cells * lon_cells
    flat_conv = conv_out.reshape(channels, cells)
    flat_field = state_field.reshape(channels, cells)
    flat_cot = cotangent.reshape(channels, cells)
    mask_float = ocean_mask.astype(jnp.float32)
    flat_mask = mask_float.reshape(1, cells)
    out_flat, grad_flat, acc_in, acc_out = fused_mlp(
        flat_conv, flat_field, flat_cot, flat_mask,
        inward_weight, inward_bias, outward_weight, layer_scale,
    )
    output_field = out_flat.reshape(channels, lat_cells, lon_cells)
    conv_grad = grad_flat.reshape(channels, lat_cells, lon_cells)
    kernel_local = kernel_terms(conv_grad, padded) * factor
    parts = (acc_in * factor, acc_out * factor, kernel_local)
    flat = jnp.concatenate([part.reshape(-1) for part in parts])
    total = flat.shape[0]
    padded_total = -(-total // 2048) * 2048
    flat = jnp.pad(flat, (0, padded_total - total))
    flat = butterfly_sum(flat, BUTTERFLY_STEPS)
    sums = []
    start = 0
    for part in parts:
        sums.append(flat[start : start + part.size].reshape(part.shape))
        start += part.size
    inward_grad, outward_grad, kernel_grad = sums
    grad_padded = extend(conv_grad)
    masked_grad = mask_float[None, :, :] * cotangent.astype(jnp.float32)
    field_grad = (masked_grad + depthwise(grad_padded, kernel, True)).astype(jnp.bfloat16)
    return (output_field, field_grad, kernel_grad, inward_grad, outward_grad)


def solution(mesh):
    in_specs = (P(None, "gy", "gx"), P(None, "gy", "gx"), P("gy", "gx"), P(), P(), P(), P(), P())
    out_specs = (P(None, "gy", "gx"), P(None, "gy", "gx"), P(), P(), P())
    return jax.shard_map(
        per_device, mesh=mesh, in_specs=in_specs, out_specs=out_specs, check_vma=False
    )
```

```python
import math

import jax
import jax.numpy as jnp
from jax import lax
from jax.sharding import PartitionSpec as P
from jax.experimental import pallas as pl
from jax.experimental.pallas import tpu as pltpu


def padded_2(block, sides, width, periodic):
    for axis, dim in sides:
        count = lax.axis_size(axis)
        forward = [(i, i + 1) for i in range(count - 1)]
        if periodic:
            forward.append((count - 1, 0))
        backward = [(target, source) for source, target in forward]
        low = lax.ppermute(
            lax.slice_in_dim(block, block.shape[dim] - width, None, axis=dim), axis, forward
        )
        high = lax.ppermute(lax.slice_in_dim(block, 0, width, axis=dim), axis, backward)
        block = jnp.concatenate([low, block, high], axis=dim)
    return block


def from_partner(block, axis, distance):
    count = lax.axis_size(axis)
    route = []
    for low in range(count):
        high = low | 1 << distance
        if high != low and high < count:
            route += [(low, high), (high, low)]
    return lax.ppermute(block, axis, route)


BUTTERFLY_STEPS = (
    ("gx", 0), ("gy", 0), ("gx", 1), ("gx", 2), ("gy", 1), ("gx", 3), ("gy", 2), ("gy", 3)
)


def butterfly_sum(flat, steps):
    trail = []
    for axis, bit in steps:
        if 1 << bit >= lax.axis_size(axis):
            continue
        count = lax.axis_size(axis)
        mine = (lax.axis_index(axis) >> bit) & 1
        pairs = [(i, i ^ (1 << bit)) for i in range(count)]
        half = flat.shape[0] // 2
        low, high = flat[:half], flat[half:]
        sent = jnp.where(mine == 0, high, low)
        kept = jnp.where(mine == 0, low, high)
        flat = kept + lax.ppermute(sent, axis, pairs)
        trail.append((axis, mine, pairs))
    for axis, mine, pairs in reversed(trail):
        other = lax.ppermute(flat, axis, pairs)
        flat = jnp.where(
            mine == 0, jnp.concatenate([flat, other]), jnp.concatenate([other, flat])
        )
    return flat


def gelu_value(values):
    return 0.5 * values * (1.0 + jax.scipy.special.erf(values / math.sqrt(2.0)))


def gelu_slope(values):
    return 0.5 * (1.0 + jax.scipy.special.erf(values / math.sqrt(2.0))) + values * jnp.exp(
        -0.5 * values * values
    ) / math.sqrt(2.0 * math.pi)


def extend(source):
    lat_cells = source.shape[1]
    wrapped = padded_2(source, (("gx", 2),), 3, True)
    extended = padded_2(wrapped, (("gy", 1),), 3, False)
    top_strip = wrapped[:, lat_cells - 3 :, :]
    count = lax.axis_size("gx")
    facing = lax.ppermute(top_strip, "gx", [(i, count - 1 - i) for i in range(count)])
    folded = jnp.flip(facing, (1, 2))
    at_top = lax.axis_index("gy") == lax.axis_size("gy") - 1
    upper_rows = jnp.where(at_top, folded, extended[:, lat_cells + 3 :, :])
    return jnp.concatenate([extended[:, : lat_cells + 3, :], upper_rows], axis=1)


def depthwise(padded, kernel, flipped):
    lat_cells = padded.shape[1] - 6
    lon_cells = padded.shape[2] - 6
    summed = jnp.zeros((padded.shape[0], lat_cells, lon_cells), jnp.float32)
    for row_tap in range(7):
        for col_tap in range(7):
            if flipped:
                weights = kernel[:, 6 - row_tap, 6 - col_tap]
            else:
                weights = kernel[:, row_tap, col_tap]
            window = padded[:, row_tap : row_tap + lat_cells, col_tap : col_tap + lon_cells].astype(
                jnp.float32
            )
            summed = summed + weights[:, None, None] * window
    return summed


def kernel_terms(grad_half, padded):
    lat_cells = grad_half.shape[1]
    lon_cells = grad_half.shape[2]
    grad_float = grad_half.astype(jnp.float32)
    row_sums = []
    for row_tap in range(7):
        column_sums = []
        for col_tap in range(7):
            window = padded[:, row_tap : row_tap + lat_cells, col_tap : col_tap + lon_cells].astype(
                jnp.float32
            )
            column_sums.append(jnp.sum(grad_float * window, axis=(1, 2)))
        row_sums.append(jnp.stack(column_sums, axis=1))
    return jnp.stack(row_sums, axis=1)


def mlp_block(
    conv_out, field_blk, cot_blk, mask_blk, inward_weight, inward_bias, outward_weight, layer_scale
):
    average = jnp.mean(conv_out, axis=0, keepdims=True)
    centered = conv_out - average
    variance = jnp.mean(centered * centered, axis=0, keepdims=True)
    inverse = lax.rsqrt(variance + 1e-06)
    normed = centered * inverse
    normed_half = normed.astype(jnp.bfloat16)
    contract = (((0,), (0,)), ((), ()))
    pre_act = (
        lax.dot_general(inward_weight, normed_half, contract, preferred_element_type=jnp.float32)
        + inward_bias[:, None]
    )
    hidden = gelu_value(pre_act).astype(jnp.bfloat16)
    branch = lax.dot_general(outward_weight, hidden, contract, preferred_element_type=jnp.float32)
    output_blk = (
        mask_blk * (field_blk.astype(jnp.float32) + layer_scale[:, None] * branch)
    ).astype(jnp.bfloat16)
    masked_grad = mask_blk * cot_blk.astype(jnp.float32)
    branch_grad = (layer_scale[:, None] * masked_grad).astype(jnp.bfloat16)
    rows_contract = (((1,), (1,)), ((), ()))
    outward_part = lax.dot_general(
        hidden, branch_grad, rows_contract, preferred_element_type=jnp.float32
    )
    hidden_grad = jnp.dot(outward_weight, branch_grad, preferred_element_type=jnp.float32)
    pre_grad = (hidden_grad * gelu_slope(pre_act)).astype(jnp.bfloat16)
    inward_part = lax.dot_general(
        normed_half, pre_grad, rows_contract, preferred_element_type=jnp.float32
    )
    normed_grad = jnp.dot(inward_weight, pre_grad, preferred_element_type=jnp.float32)
    mean_grad = jnp.mean(normed_grad, axis=0, keepdims=True)
    mean_prod = jnp.mean(normed_grad * normed, axis=0, keepdims=True)
    conv_grad = (inverse * (normed_grad - mean_grad - normed * mean_prod)).astype(jnp.bfloat16)
    return (output_blk, conv_grad, inward_part, outward_part)


TILE = 256


def mlp_kernel(
    conv_ref, field_ref, cot_ref, mask_ref, win_t_ref, win_ref, wout_ref, wout_t_ref,
    bias_ref, scale_ref, out_ref, grad_ref, acc_in_ref, acc_out_ref,
):
    @pl.when(pl.program_id(0) == 0)
    def _():
        acc_in_ref[...] = jnp.zeros_like(acc_in_ref)
        acc_out_ref[...] = jnp.zeros_like(acc_out_ref)

    conv = conv_ref[...]
    channels = conv.shape[0]
    average = jnp.sum(conv, axis=0, keepdims=True) / channels
    centered = conv - average
    variance = jnp.sum(centered * centered, axis=0, keepdims=True) / channels
    inverse = lax.rsqrt(variance + 1e-06)
    normed = centered * inverse
    normed_half = normed.astype(jnp.bfloat16)
    pre_act = jnp.dot(win_t_ref[...], normed_half, preferred_element_type=jnp.float32)
    pre_act = pre_act + bias_ref[...]
    hidden = gelu_value(pre_act).astype(jnp.bfloat16)
    branch = jnp.dot(wout_t_ref[...], hidden, preferred_element_type=jnp.float32)
    mask = mask_ref[...]
    scale = scale_ref[...]
    out_ref[...] = (
        mask * (field_ref[...].astype(jnp.float32) + scale * branch)
    ).astype(out_ref.dtype)
    masked_grad = mask * cot_ref[...].astype(jnp.float32)
    branch_grad = (scale * masked_grad).astype(jnp.bfloat16)
    rows_contract = (((1,), (1,)), ((), ()))
    acc_out_ref[...] += lax.dot_general(
        hidden, branch_grad, rows_contract, preferred_element_type=jnp.float32
    )
    hidden_grad = jnp.dot(wout_ref[...], branch_grad, preferred_element_type=jnp.float32)
    pre_grad = (hidden_grad * gelu_slope(pre_act)).astype(jnp.bfloat16)
    acc_in_ref[...] += lax.dot_general(
        normed_half, pre_grad, rows_contract, preferred_element_type=jnp.float32
    )
    normed_grad = jnp.dot(win_ref[...], pre_grad, preferred_element_type=jnp.float32)
    mean_grad = jnp.sum(normed_grad, axis=0, keepdims=True) / channels
    mean_prod = jnp.sum(normed_grad * normed, axis=0, keepdims=True) / channels
    grad_ref[...] = (inverse * (normed_grad - mean_grad - normed * mean_prod)).astype(
        grad_ref.dtype
    )


def fused_mlp(conv, field, cot, mask, inward_weight, inward_bias, outward_weight, layer_scale):
    channels, cells = conv.shape
    hidden_units = inward_weight.shape[1]
    tile = TILE if cells % TILE == 0 else cells
    steps = cells // tile
    cell_block = lambda rows: pl.BlockSpec((rows, tile), lambda i: (0, i))
    whole = lambda shape: pl.BlockSpec(shape, lambda i: (0, 0))
    flops = 2 * 6 * channels * hidden_units * cells
    return pl.pallas_call(
        mlp_kernel,
        grid=(steps,),
        in_specs=[
            cell_block(channels), cell_block(channels), cell_block(channels), cell_block(1),
            whole((hidden_units, channels)), whole((channels, hidden_units)),
            whole((hidden_units, channels)), whole((channels, hidden_units)),
            whole((hidden_units, 1)), whole((channels, 1)),
        ],
        out_specs=[
            cell_block(channels), cell_block(channels),
            whole((channels, hidden_units)), whole((hidden_units, channels)),
        ],
        out_shape=[
            jax.ShapeDtypeStruct((channels, cells), jnp.bfloat16),
            jax.ShapeDtypeStruct((channels, cells), jnp.bfloat16),
            jax.ShapeDtypeStruct((channels, hidden_units), jnp.float32),
            jax.ShapeDtypeStruct((hidden_units, channels), jnp.float32),
        ],
        compiler_params=pltpu.CompilerParams(dimension_semantics=("arbitrary",)),
        cost_estimate=pl.CostEstimate(
            flops=flops, transcendentals=3 * hidden_units * cells,
            bytes_accessed=channels * cells * 12,
        ),
    )(
        conv, field, cot, mask, inward_weight.T, inward_weight, outward_weight,
        outward_weight.T, inward_bias.reshape(hidden_units, 1),
        layer_scale.reshape(channels, 1),
    )


def per_device(
    state_field,
    cotangent,
    ocean_mask,
    kernel,
    inward_weight,
    inward_bias,
    outward_weight,
    layer_scale,
):
    channels, lat_cells, lon_cells = state_field.shape
    hidden_units = inward_weight.shape[1]
    factor = 1.0 / math.sqrt(lat_cells * lon_cells)
    padded = extend(state_field)
    conv_out = depthwise(padded, kernel, False)
    cells = lat_cells * lon_cells
    flat_conv = conv_out.reshape(channels, cells)
    flat_field = state_field.reshape(channels, cells)
    flat_cot = cotangent.reshape(channels, cells)
    mask_float = ocean_mask.astype(jnp.float32)
    flat_mask = mask_float.reshape(1, cells)
    out_flat, grad_flat, acc_in, acc_out = fused_mlp(
        flat_conv, flat_field, flat_cot, flat_mask,
        inward_weight, inward_bias, outward_weight, layer_scale,
    )
    output_field = out_flat.reshape(channels, lat_cells, lon_cells)
    conv_grad = grad_flat.reshape(channels, lat_cells, lon_cells)
    kernel_local = kernel_terms(conv_grad, padded) * factor
    parts = (acc_in * factor, acc_out * factor, kernel_local)
    flat = jnp.concatenate([part.reshape(-1) for part in parts])
    total = flat.shape[0]
    padded_total = -(-total // 2048) * 2048
    flat = jnp.pad(flat, (0, padded_total - total))
    flat = butterfly_sum(flat, BUTTERFLY_STEPS)
    sums = []
    start = 0
    for part in parts:
        sums.append(flat[start : start + part.size].reshape(part.shape))
        start += part.size
    inward_grad, outward_grad, kernel_grad = sums
    grad_padded = extend(conv_grad)
    masked_grad = mask_float[None, :, :] * cotangent.astype(jnp.float32)
    field_grad = (masked_grad + depthwise(grad_padded, kernel, True)).astype(jnp.bfloat16)
    return (output_field, field_grad, kernel_grad, inward_grad, outward_grad)


def solution(mesh):
    in_specs = (P(None, "gy", "gx"), P(None, "gy", "gx"), P("gy", "gx"), P(), P(), P(), P(), P())
    out_specs = (P(None, "gy", "gx"), P(None, "gy", "gx"), P(), P(), P())
    return jax.shard_map(
        per_device, mesh=mesh, in_specs=in_specs, out_specs=out_specs, check_vma=False
    )
```
